512 devices in a mesh: seq: 16 (over z), exp: 32 (over x, y, core).
Axes of the slice: x: 4, y: 4, z: 16, core: 2. Of those that a mesh axis runs over, the one named last changes fastest.
Arguments:
- queries: bfloat16 [2048, 8192], P('seq', 'exp'), may hold values from -6 to 6
- key_matrix: bfloat16 [2048, 8192], P('seq', 'exp'), may hold values from -6 to 6
- values: bfloat16 [2048, 8192], P('seq', 'exp'), may hold values from -6 to 6
- log_decay: float32 [64, 2048], P('exp', 'seq'), may hold values from -3 to 0
- residual: bfloat16 [2048, 3072], P('seq'), may hold values from -6 to 6
- out_weight: bfloat16 [3072, 8192], P('seq', 'exp'), may hold values from -0.0625 to 0.0625
- router: bfloat16 [3072, 32], replicated, may hold values from -0.109375 to 0.109375
- expert_ids: int32 [2048, 2], P('seq'), may hold values from 0 to 31, all different within a row; in each aligned block of 128 rows (0 to 127, 128 to 255, ...) at most 12 rows name the same one
- up_weight: bfloat16 [32, 3072, 4608], P('exp', None, 'seq'), may hold values from -0.109375 to 0.109375
- down_weight: bfloat16 [32, 4608, 3072], P('exp', 'seq'), may hold values from -0.09375 to 0.09375
Outputs:
- layer_out: bfloat16 [2048, 3072], P(('seq', 'exp'))
The draws below stay inside these ranges and needn't reach their ends.
Inputs may be any that keep to these rules, and one draw needn't show every extreme that they name: `expert_ids`: in each aligned block of 128 rows (one sequence block) no expert is named by more than 12 rows, a bound that some block reaches; a row names 2 different experts.
All inputs are finite; a program needn't handle non-finite values.
Results may differ from the reference program's by a relative error of at most 0.015.
Values may be sent and summed in bfloat16 or wider, within the bound.
No kernel may reach another device: no remote copies, remote signals or barrier semaphores. Data moves between devices by JAX's collectives and lax.ppermute only.
A program may use at most 64 MiB of HBM per device.

```python
import math
import jax
import jax.numpy as jnp
import numpy as np
from jax import lax

D = 3072
DH = 128
FFW = 4608
TOP = 2
BLK = 128
HEADS = 64
EXPERTS = 32
TOKENS = 2048
CAP = 12
N_SEQ = 16


def draw_log_decay(key, part):
    keys = jax.random.split(key, 6)
    slow_share = 0.5
    slow = jax.random.bernoulli(keys[0], slow_share, (HEADS, 1))
    fast_rate = jnp.exp(jax.random.uniform(keys[1], (HEADS, 1), jnp.float32, math.log(1.0 / 50.0), math.log(1.0 / 30.0)))
    slow_rate = math.log(2.5) / TOKENS * jax.random.uniform(keys[2], (HEADS, 1), jnp.float32, 0.3, 1.0)
    decay_rate = jnp.where(slow, slow_rate, fast_rate)
    coarse_estimate = jax.random.uniform(keys[3], (HEADS, TOKENS), jnp.float32, 0.5, 1.5)
    slot_locations = jax.random.randint(keys[4], (HEADS, 3), 0, TOKENS)
    layer_depth = jax.random.uniform(keys[5], (HEADS, 3), jnp.float32, math.log(0.5), math.log(0.8))
    target_locations = jnp.arange(TOKENS, dtype=jnp.int32)[None, None, :]
    sudden_spike = jnp.sum(jnp.where(target_locations == slot_locations[:, :, None], layer_depth[:, :, None], 0.0), axis=1)
    return (-decay_rate * coarse_estimate + sudden_spike).astype(jnp.float32)


def levels(rng, dims, cuts, least, largest):
    gain, own = 1.0, jax.random.fold_in(rng, 6)
    for position, shards_of in cuts:
        draws = jnp.exp(jax.random.uniform(jax.random.fold_in(own, position), (shards_of,), jnp.float32, least / len(cuts), largest / len(cuts)))
        gain = gain * jnp.repeat(draws, dims[position] // shards_of).reshape([-1 if axis == position else 1 for axis in range(len(dims))])
    return gain


def routed_block(rng, own, number, rows, count, top, reach, lean):
    sequence = jax.random.permutation(rng, count)
    crowded, ordinary = load_shares(count, rows * top, reach, lean, True), load_shares(count, rows * top, reach, lean, False)
    places = jnp.arange(count)

    def named(tallies, turn):
        used = int((tallies > 0).sum())
        fixed = max(1, used // 4)
        moved = fixed + (places - fixed + turn * (used - fixed)) % max(1, count - fixed)
        return jnp.zeros((count,), jnp.int32).at[sequence[jnp.where(places < fixed, places, moved)]].set(jnp.asarray(tallies, jnp.int32))

    tallies = jnp.where(number % 4 == 0, named(crowded, number // 4), named(ordinary, number - number // 4 - 1))
    mixed = jax.random.permutation(jax.random.fold_in(own, 3), count)
    source_of, taker = mixed[0:count // 2 * 2:2], mixed[1:count // 2 * 2:2]
    slack = jnp.minimum(tallies[source_of] - 1, reach - tallies[taker]) // 2
    slack = jnp.where((source_of == sequence[0]) | (taker == sequence[0]) | (tallies[taker] == 0), 0, jnp.maximum(slack, 0))
    moved = jax.random.randint(jax.random.fold_in(own, 4), (count // 2,), 0, 1 << 20) % (slack + 1)
    tallies = tallies.at[source_of].add(-moved).at[taker].add(moved)
    labels = jnp.searchsorted(jnp.cumsum(tallies), jnp.arange(rows * top), side="right").astype(jnp.int32)
    grid = labels.reshape(top, rows).T
    grid = grid[jax.random.permutation(jax.random.fold_in(own, 1), rows)]
    turn = jax.random.randint(jax.random.fold_in(own, 2), (rows, 1), 0, top)
    return jnp.take_along_axis(grid, (jnp.arange(top)[None, :] + turn) % top, axis=1)


def load_shares(number_of, total, most, slope, full):
    weights = [(1 << 20) // math.isqrt(grade ** slope) + 1 for grade in range(1, number_of + 1)]
    largest = most if full else min(most, max(-(-total // number_of), total * weights[0] // sum(weights)))
    least = 1 if total - largest >= number_of - 1 else 0
    holding, spare = [largest] + [least] * (number_of - 1), total - largest - least * (number_of - 1)
    while spare > 0:
        free = [i for i in range(1, number_of) if holding[i] < largest] or [i for i in range(1, number_of) if holding[i] < most]
        mass, budget = sum([weights[i] for i in free]), spare
        for i in free:
            more = min(most - holding[i], max(1, budget * weights[i] // mass), spare)
            holding[i] = holding[i] + more
            spare = spare - more
    return np.array(holding)


def centred(rng, dims, spread, bound, cuts=(), kind=jnp.bfloat16):
    values = spread * jax.random.normal(rng, dims, jnp.float32)
    if cuts:
        values = values * levels(rng, dims, cuts, -0.22, 0.18)
    return jnp.clip(values, -bound, bound).astype(kind)


def setup_inputs(seed: int = 0) -> dict:
    splits = jax.random.split(jax.random.key(seed), 11)
    queries = centred(splits[0], (TOKENS, HEADS * DH), 1.0, 6.0, ((0, 16), (1, 32)))
    key_matrix = centred(splits[1], (TOKENS, HEADS * DH), 1.0, 6.0, ((0, 16), (1, 32)))
    values = centred(splits[2], (TOKENS, HEADS * DH), 1.0, 6.0, ((0, 16), (1, 32)))
    log_decay = draw_log_decay(jax.random.fold_in(splits[10], 71), 0)
    residual = centred(splits[4], (TOKENS, D), 1.0, 6.0, ((0, 16),))
    out_weight = centred(splits[5], (D, HEADS * DH), (HEADS * DH) ** -0.5, 0.0625, ((0, 16), (1, 32)))
    router = centred(splits[6], (D, EXPERTS), D ** -0.5, 0.109375)
    expert_ids_keys = jax.random.split(jax.random.fold_in(splits[7], 1), TOKENS // BLK)
    expert_ids_turns = jax.random.permutation(jax.random.fold_in(splits[7], 3), TOKENS // BLK)
    expert_ids = jax.vmap(lambda own, number: routed_block(jax.random.fold_in(splits[7], 2), own, number, BLK, EXPERTS, TOP, CAP, 2))(expert_ids_keys, expert_ids_turns).reshape((TOKENS, TOP))
    up_weight = centred(splits[8], (EXPERTS, D, FFW), D ** -0.5, 0.109375, ((0, 32), (2, 16)))
    down_weight = centred(splits[9], (EXPERTS, FFW, D), FFW ** -0.5, 0.09375, ((0, 32), (1, 16)))
    return {"queries": queries, "key_matrix": key_matrix, "values": values, "log_decay": log_decay, "residual": residual, "out_weight": out_weight, "router": router, "expert_ids": expert_ids, "up_weight": up_weight, "down_weight": down_weight}


def block_step(state, inputs):
    qb, kb, vb, gb = inputs
    cum = jnp.cumsum(gb, axis=1)
    last = cum[:, -1:]
    size = gb.shape[1]
    lower = jnp.arange(size)[:, None] >= jnp.arange(size)[None, :]
    diff = cum[:, :, None] - cum[:, None, :]
    weight = jnp.where(lower[None], jnp.exp(jnp.where(lower[None], diff, 0.0)), 0.0)
    scores = jnp.einsum('hid,hjd->hij', qb, kb, precision=lax.Precision.HIGHEST) * weight
    inner = jnp.einsum('hij,hjd->hid', scores, vb, precision=lax.Precision.HIGHEST)
    outer = jnp.exp(cum)[:, :, None] * jnp.einsum('hid,hde->hie', qb, state, precision=lax.Precision.HIGHEST)
    kscaled = kb * jnp.exp(last - cum)[:, :, None]
    fresh = jnp.exp(last)[:, :, None] * state + jnp.einsum('hjd,hje->hde', kscaled, vb, precision=lax.Precision.HIGHEST)
    return (fresh, inner + outer)

def run_expert(operands):
    rows_e, up_e, down_e = operands
    hidden = jax.nn.silu(jnp.dot(rows_e, up_e, preferred_element_type=jnp.float32)).astype(jnp.bfloat16)
    return jnp.dot(hidden, down_e, preferred_element_type=jnp.float32)

def reference(queries, key_matrix, values, log_decay, residual, out_weight, router, expert_ids, up_weight, down_weight):

    def split_heads(array):
        return array.astype(jnp.float32).reshape(N_SEQ, BLK, HEADS, DH).transpose(0, 2, 1, 3)
    qall = split_heads(queries)
    kall = split_heads(key_matrix)
    vall = split_heads(values)
    decay = log_decay.reshape(HEADS, N_SEQ, BLK).transpose(1, 0, 2)
    start = jnp.zeros((HEADS, DH, DH), jnp.float32)
    _, mixed = lax.scan(block_step, start, (qall, kall, vall, decay))
    mixed = mixed * lax.rsqrt(lax.optimization_barrier(jnp.mean(mixed * mixed, axis=-1, keepdims=True)) + 1e-06)
    attn = mixed.transpose(0, 2, 1, 3).reshape(TOKENS, HEADS * DH).astype(jnp.bfloat16)
    projected = lax.dot_general(attn, out_weight, (((1,), (1,)), ((), ())), preferred_element_type=jnp.float32)
    stream = residual.astype(jnp.float32)
    normed = (stream * lax.rsqrt(lax.optimization_barrier(jnp.mean(stream * stream, axis=-1, keepdims=True)) + 1e-05)).astype(jnp.bfloat16)
    logits = jnp.dot(normed, router, preferred_element_type=jnp.float32)
    chosen = jnp.take_along_axis(logits, expert_ids, axis=1)
    score = jax.nn.sigmoid(chosen)
    gates = score / lax.optimization_barrier(jnp.sum(score, axis=1, keepdims=True))
    grouped = expert_ids.reshape(N_SEQ, BLK * TOP)
    onehot = (grouped[:, :, None] == jnp.arange(EXPERTS, dtype=jnp.int32)[None, None, :]).astype(jnp.int32)
    ranks = jnp.cumsum(onehot, axis=1) - onehot
    slot = lax.optimization_barrier(jnp.sum(ranks * onehot, axis=-1)).reshape(-1).astype(jnp.int32)
    flat_ids = expert_ids.reshape(-1).astype(jnp.int32)
    route = jnp.arange(TOKENS * TOP, dtype=jnp.int32)
    token_index = route // TOP
    row_index = token_index // BLK * CAP + slot
    buffer = jnp.zeros((EXPERTS, N_SEQ * CAP, D), jnp.bfloat16)
    buffer = buffer.at[flat_ids, row_index].set(normed[token_index])
    outputs = lax.map(run_expert, (buffer, up_weight, down_weight))
    picked = outputs[flat_ids, row_index].reshape(TOKENS, TOP, D)
    combined = lax.optimization_barrier(jnp.sum(gates[:, :, None] * picked, axis=1))
    return (stream + projected + combined).astype(jnp.bfloat16)
```

```python
import jax
import jax.numpy as jnp
from jax import lax
from jax.sharding import PartitionSpec as P


def halving_scatter(x, axis):
    n = x.shape[0]
    me = lax.axis_index(axis)
    buf = x
    for k in range(n.bit_length() - 1):
        half = buf.reshape(buf.shape[0] // 2, 2, *buf.shape[1:])
        upper = ((me >> k) & 1) == 1
        keep = jnp.where(upper, half[:, 1], half[:, 0])
        send = jnp.where(upper, half[:, 0], half[:, 1])
        got = lax.ppermute(send, axis, [(i, i ^ (1 << k)) for i in range(n)])
        buf = keep + got
    return buf[0]


def shards(
    queries,
    key_matrix,
    values,
    log_decay,
    residual,
    out_weight,
    router,
    expert_ids,
    up_weight,
    down_weight,
):
    rows = queries.shape[0]
    heads_here = log_decay.shape[0]
    width = queries.shape[1] // heads_here
    n_seq = lax.axis_size("seq")
    n_exp = lax.axis_size("exp")
    me_seq = lax.axis_index("seq")
    owner = lax.axis_index("exp")

    def split_heads(array):
        return array.astype(jnp.float32).reshape(rows, heads_here, width).transpose(1, 0, 2)

    qloc = split_heads(queries)
    kloc = split_heads(key_matrix)
    vloc = split_heads(values)
    cum = jnp.cumsum(log_decay, axis=1)
    last = cum[:, -1:]
    carry_decay = jnp.exp(last[:, 0])
    kscaled = kloc * jnp.exp(last - cum)[:, :, None]
    local_state = jnp.einsum("hjd,hje->hde", kscaled, vloc, precision=lax.Precision.HIGHEST)

    stream = residual.astype(jnp.float32)
    normed = (stream * lax.rsqrt(jnp.mean(stream * stream, axis=-1, keepdims=True) + 1e-05)).astype(
        jnp.bfloat16
    )
    logits = jnp.dot(normed, router, preferred_element_type=jnp.float32)
    count_experts = router.shape[1]
    select_experts = (
        expert_ids[:, :, None] == jnp.arange(count_experts, dtype=jnp.int32)[None, None, :]
    )
    chosen = jnp.sum(jnp.where(select_experts, logits[:, None, :], 0.0), axis=-1)
    score = jax.nn.sigmoid(chosen)
    gates = score / jnp.sum(score, axis=1, keepdims=True)
    topk = expert_ids.shape[1]
    capacity = 3 * rows * topk // (2 * n_exp)
    mine = (expert_ids.reshape(-1) == owner).astype(jnp.int32)
    ranks = jnp.cumsum(mine) - mine
    slot_pick = (ranks[None, :] == jnp.arange(capacity, dtype=jnp.int32)[:, None]) & (
        mine[None, :] == 1
    )
    slot_pick = slot_pick.astype(jnp.float32).reshape(capacity, rows, topk)
    token_pick = jnp.sum(slot_pick, axis=2).astype(jnp.bfloat16)
    slot_rows = jnp.dot(token_pick, normed, preferred_element_type=jnp.float32).astype(jnp.bfloat16)

    decay_hi = carry_decay.astype(jnp.bfloat16)
    decay_lo = (carry_decay - decay_hi.astype(jnp.float32)).astype(jnp.bfloat16)
    lane = 128
    pieces = [
        local_state.astype(jnp.bfloat16).reshape(-1),
        slot_rows.reshape(-1),
        out_weight.reshape(-1),
        jnp.pad(jnp.concatenate([decay_hi, decay_lo]), (0, lane - 2 * heads_here)),
    ]
    sizes = [p.shape[0] for p in pieces]
    flat = jnp.concatenate(pieces)
    total = flat.shape[0]
    padded = -(-total // (16 * lane)) * (16 * lane)
    flat = jnp.pad(flat, (0, padded - total)).reshape(padded // lane, lane)
    gathered = lax.all_gather(flat, "seq", axis=0, tiled=False).reshape(n_seq, padded)
    offsets = [sum(sizes[:i]) for i in range(len(sizes))]
    states = gathered[:, offsets[0] : offsets[0] + sizes[0]].reshape(n_seq, heads_here, width, width)
    gathered_rows = gathered[:, offsets[1] : offsets[1] + sizes[1]].reshape(
        n_seq * capacity, normed.shape[1]
    )
    full_weight = gathered[:, offsets[2] : offsets[2] + sizes[2]].reshape(
        n_seq * out_weight.shape[0], out_weight.shape[1]
    )
    decays = gathered[:, offsets[3] : offsets[3] + 2 * heads_here].astype(jnp.float32)
    decays = decays[:, :heads_here] + decays[:, heads_here:]

    blocks = jnp.arange(n_seq)
    between = (blocks[:, None] < blocks[None, :]) & (blocks[None, :] < me_seq)
    factors = jnp.where(between[:, :, None], decays[None, :, :], 1.0)
    reach = jnp.where((blocks < me_seq)[:, None], jnp.prod(factors, axis=1), 0.0)
    state_in = jnp.einsum(
        "jh,jhde->hde", reach, states.astype(jnp.float32), precision=lax.Precision.HIGHEST
    )

    lower = jnp.arange(rows)[:, None] >= jnp.arange(rows)[None, :]
    diff = cum[:, :, None] - cum[:, None, :]
    weight = jnp.where(lower[None], jnp.exp(jnp.where(lower[None], diff, 0.0)), 0.0)
    scores = jnp.einsum("hid,hjd->hij", qloc, kloc, precision=lax.Precision.HIGHEST) * weight
    inner = jnp.einsum("hij,hjd->hid", scores, vloc, precision=lax.Precision.HIGHEST)
    outer = jnp.exp(cum)[:, :, None] * jnp.einsum(
        "hid,hde->hie", qloc, state_in, precision=lax.Precision.HIGHEST
    )
    mixed = inner + outer
    mixed = mixed * lax.rsqrt(jnp.mean(mixed * mixed, axis=-1, keepdims=True) + 1e-06)
    attn = mixed.transpose(1, 0, 2).reshape(rows, heads_here * width).astype(jnp.bfloat16)

    projected = lax.dot_general(
        attn, full_weight, (((1,), (1,)), ((), ())), preferred_element_type=jnp.float32
    )
    hidden = jax.nn.silu(
        jnp.dot(gathered_rows, up_weight[0], preferred_element_type=jnp.float32)
    ).astype(jnp.bfloat16)
    expert_part = jnp.dot(hidden, down_weight[0], preferred_element_type=jnp.float32)
    expert_out = lax.psum_scatter(
        expert_part.astype(jnp.bfloat16).reshape(n_seq, capacity, -1),
        "seq",
        scatter_dimension=0,
        tiled=True,
    )[0].astype(jnp.float32)
    combine = jnp.einsum("cbk,bk->bc", slot_pick, gates, precision=lax.Precision.HIGHEST)
    contribution = jnp.dot(combine, expert_out, precision=lax.Precision.HIGHEST)
    partial = (projected + contribution).reshape(n_exp, rows // n_exp, -1)
    summed = halving_scatter(partial, "exp")
    own_rows = summed.shape[0]
    own = lax.dynamic_slice_in_dim(stream, owner * own_rows, own_rows, 0)
    return (own + summed).astype(jnp.bfloat16)


def solution(mesh):
    in_specs = (
        P("seq", "exp"),
        P("seq", "exp"),
        P("seq", "exp"),
        P("exp", "seq"),
        P("seq", None),
        P("seq", "exp"),
        P(),
        P("seq", None),
        P("exp", None, "seq"),
        P("exp", "seq", None),
    )
    out_specs = P(("seq", "exp"), None)
    return jax.shard_map(shards, mesh=mesh, in_specs=in_specs, out_specs=out_specs, check_vma=False)
```

```python
import jax
import jax.numpy as jnp
from jax import lax
from jax.sharding import PartitionSpec as P


def halving_scatter(x, axis):
    n = x.shape[0]
    me = lax.axis_index(axis)
    buf = x
    for k in range(n.bit_length() - 1):
        half = buf.reshape(buf.shape[0] // 2, 2, *buf.shape[1:])
        upper = ((me >> k) & 1) == 1
        keep = jnp.where(upper, half[:, 1], half[:, 0])
        send = jnp.where(upper, half[:, 0], half[:, 1])
        got = lax.ppermute(send.astype(jnp.bfloat16), axis, [(i, i ^ (1 << k)) for i in range(n)])
        buf = keep + got.astype(keep.dtype)
    return buf[0]


def shards(
    queries,
    key_matrix,
    values,
    log_decay,
    residual,
    out_weight,
    router,
    expert_ids,
    up_weight,
    down_weight,
):
    rows = queries.shape[0]
    heads_here = log_decay.shape[0]
    width = queries.shape[1] // heads_here
    n_seq = lax.axis_size("seq")
    n_exp = lax.axis_size("exp")
    me_seq = lax.axis_index("seq")
    owner = lax.axis_index("exp")

    def split_heads(array):
        return array.astype(jnp.float32).reshape(rows, heads_here, width).transpose(1, 0, 2)

    qloc = split_heads(queries)
    kloc = split_heads(key_matrix)
    vloc = split_heads(values)
    cum = jnp.cumsum(log_decay, axis=1)
    last = cum[:, -1:]
    carry_decay = jnp.exp(last[:, 0])
    kscaled = kloc * jnp.exp(last - cum)[:, :, None]
    local_state = jnp.einsum("hjd,hje->hde", kscaled, vloc, precision=lax.Precision.HIGHEST)

    stream = residual.astype(jnp.float32)
    normed = (stream * lax.rsqrt(jnp.mean(stream * stream, axis=-1, keepdims=True) + 1e-05)).astype(
        jnp.bfloat16
    )
    logits = jnp.dot(normed, router, preferred_element_type=jnp.float32)
    count_experts = router.shape[1]
    select_experts = (
        expert_ids[:, :, None] == jnp.arange(count_experts, dtype=jnp.int32)[None, None, :]
    )
    chosen = jnp.sum(jnp.where(select_experts, logits[:, None, :], 0.0), axis=-1)
    score = jax.nn.sigmoid(chosen)
    gates = score / jnp.sum(score, axis=1, keepdims=True)
    topk = expert_ids.shape[1]
    capacity = 3 * rows * topk // (2 * n_exp)
    slots = -(-capacity // 16) * 16
    mine = (expert_ids.reshape(-1) == owner).astype(jnp.int32)
    ranks = jnp.cumsum(mine) - mine
    slot_pick = (ranks[None, :] == jnp.arange(slots, dtype=jnp.int32)[:, None]) & (
        mine[None, :] == 1
    )
    slot_pick = slot_pick.astype(jnp.float32).reshape(slots, rows, topk)
    token_pick = jnp.sum(slot_pick, axis=2).astype(jnp.bfloat16)
    slot_rows = jnp.dot(token_pick, normed, preferred_element_type=jnp.float32).astype(jnp.bfloat16)

    model = normed.shape[1]
    decay_hi = carry_decay.astype(jnp.bfloat16)
    decay_lo = (carry_decay - decay_hi.astype(jnp.float32)).astype(jnp.bfloat16)

    def as_slab(v):
        v = v.reshape(-1)
        r = -(-v.shape[0] // model)
        return jnp.pad(v, (0, r * model - v.shape[0])).reshape(r, model)

    pieces = [
        slot_rows,
        as_slab(out_weight),
        as_slab(local_state.astype(jnp.bfloat16)),
        as_slab(jnp.concatenate([decay_hi, decay_lo])),
    ]
    sizes = [p.shape[0] for p in pieces]
    slab = jnp.concatenate(pieces)
    total = slab.shape[0]
    padded = -(-total // 16) * 16
    slab = jnp.pad(slab, ((0, padded - total), (0, 0)))
    gathered = lax.all_gather(slab, "seq", axis=0, tiled=False)
    offsets = [sum(sizes[:i]) for i in range(len(sizes))]
    gathered_rows = gathered[:, offsets[0] : offsets[0] + sizes[0]].reshape(n_seq * slots, model)
    full_weight = (
        gathered[:, offsets[1] : offsets[1] + sizes[1]]
        .reshape(n_seq, -1)[:, : out_weight.size]
        .reshape(n_seq * out_weight.shape[0], out_weight.shape[1])
    )
    states = (
        gathered[:, offsets[2] : offsets[2] + sizes[2]]
        .reshape(n_seq, -1)[:, : local_state.size]
        .reshape(n_seq, heads_here, width, width)
    )
    decays = gathered[:, offsets[3], : 2 * heads_here].astype(jnp.float32)
    decays = decays[:, :heads_here] + decays[:, heads_here:]

    blocks = jnp.arange(n_seq)
    between = (blocks[:, None] < blocks[None, :]) & (blocks[None, :] < me_seq)
    factors = jnp.where(between[:, :, None], decays[None, :, :], 1.0)
    reach = jnp.where((blocks < me_seq)[:, None], jnp.prod(factors, axis=1), 0.0)
    state_in = jnp.einsum(
        "jh,jhde->hde", reach, states.astype(jnp.float32), precision=lax.Precision.HIGHEST
    )

    lower = jnp.arange(rows)[:, None] >= jnp.arange(rows)[None, :]
    diff = cum[:, :, None] - cum[:, None, :]
    weight = jnp.where(lower[None], jnp.exp(jnp.where(lower[None], diff, 0.0)), 0.0)
    scores = jnp.einsum("hid,hjd->hij", qloc, kloc, precision=lax.Precision.HIGHEST) * weight
    inner = jnp.einsum("hij,hjd->hid", scores, vloc, precision=lax.Precision.HIGHEST)
    outer = jnp.exp(cum)[:, :, None] * jnp.einsum(
        "hid,hde->hie", qloc, state_in, precision=lax.Precision.HIGHEST
    )
    mixed = inner + outer
    mixed = mixed * lax.rsqrt(jnp.mean(mixed * mixed, axis=-1, keepdims=True) + 1e-06)
    attn = mixed.transpose(1, 0, 2).reshape(rows, heads_here * width).astype(jnp.bfloat16)

    projected = lax.dot_general(
        attn, full_weight, (((1,), (1,)), ((), ())), preferred_element_type=jnp.float32
    )
    hidden = jax.nn.silu(
        jnp.dot(gathered_rows, up_weight[0], preferred_element_type=jnp.float32)
    ).astype(jnp.bfloat16)
    expert_part = jnp.dot(hidden, down_weight[0], preferred_element_type=jnp.float32)
    expert_out = lax.psum_scatter(
        expert_part.astype(jnp.bfloat16).reshape(n_seq, slots, -1),
        "seq",
        scatter_dimension=0,
        tiled=True,
    )[0].astype(jnp.float32)
    combine = jnp.einsum("cbk,bk->bc", slot_pick, gates, precision=lax.Precision.HIGHEST)
    contribution = jnp.dot(combine, expert_out, precision=lax.Precision.HIGHEST)
    partial = (projected + contribution).reshape(n_exp, rows // n_exp, -1)
    summed = halving_scatter(partial, "exp")
    own_rows = summed.shape[0]
    own = lax.dynamic_slice_in_dim(stream, owner * own_rows, own_rows, 0)
    return (own + summed).astype(jnp.bfloat16)


def solution(mesh):
    in_specs = (
        P("seq", "exp"),
        P("seq", "exp"),
        P("seq", "exp"),
        P("exp", "seq"),
        P("seq", None),
        P("seq", "exp"),
        P(),
        P("seq", None),
        P("exp", None, "seq"),
        P("exp", "seq", None),
    )
    out_specs = P(("seq", "exp"), None)
    return jax.shard_map(shards, mesh=mesh, in_specs=in_specs, out_specs=out_specs, check_vma=False)
```

```python
import jax
import jax.numpy as jnp
from jax import lax
from jax.sharding import PartitionSpec as P


def halving_scatter(x, axis):
    n = x.shape[0]
    me = lax.axis_index(axis)
    buf = x
    for k in range(n.bit_length() - 1):
        half = buf.reshape(buf.shape[0] // 2, 2, *buf.shape[1:])
        upper = ((me >> k) & 1) == 1
        keep = jnp.where(upper, half[:, 1], half[:, 0])
        send = jnp.where(upper, half[:, 0], half[:, 1])
        got = lax.ppermute(send.astype(jnp.bfloat16), axis, [(i, i ^ (1 << k)) for i in range(n)])
        buf = keep + got.astype(keep.dtype)
    return buf[0]


def ring_scatter(parts, axis):
    n = parts.shape[0]
    me = lax.axis_index(axis)
    half = n // 2
    right = [(i, (i + 1) % n) for i in range(n)]
    left = [(i, (i - 1) % n) for i in range(n)]

    def block(offset):
        return lax.dynamic_index_in_dim(parts, (me + offset + n) % n, 0, keepdims=False)

    cw = None
    ccw = None
    for k in range(1, half + 1):
        m_ccw = block(k - 1 - half)
        if ccw is not None:
            m_ccw = m_ccw + ccw.astype(m_ccw.dtype)
        if k < half:
            m_cw = block(half - k)
            if cw is not None:
                m_cw = m_cw + cw.astype(m_cw.dtype)
            m_ccw, m_cw = lax.optimization_barrier((m_ccw.astype(jnp.bfloat16), m_cw.astype(jnp.bfloat16)))
            cw = lax.ppermute(m_cw, axis, right)
        ccw = lax.ppermute(m_ccw.astype(jnp.bfloat16), axis, left)
    return block(0) + cw.astype(parts.dtype) + ccw.astype(parts.dtype)


def shards(
    queries,
    key_matrix,
    values,
    log_decay,
    residual,
    out_weight,
    router,
    expert_ids,
    up_weight,
    down_weight,
):
    rows = queries.shape[0]
    heads_here = log_decay.shape[0]
    width = queries.shape[1] // heads_here
    n_seq = lax.axis_size("seq")
    n_exp = lax.axis_size("exp")
    me_seq = lax.axis_index("seq")
    owner = lax.axis_index("exp")

    def split_heads(array):
        return array.astype(jnp.float32).reshape(rows, heads_here, width).transpose(1, 0, 2)

    qloc = split_heads(queries)
    kloc = split_heads(key_matrix)
    vloc = split_heads(values)
    cum = jnp.cumsum(log_decay, axis=1)
    last = cum[:, -1:]
    carry_decay = jnp.exp(last[:, 0])
    kscaled = kloc * jnp.exp(last - cum)[:, :, None]
    local_state = jnp.einsum("hjd,hje->hde", kscaled, vloc, precision=lax.Precision.HIGHEST)

    stream = residual.astype(jnp.float32)
    normed = (stream * lax.rsqrt(jnp.mean(stream * stream, axis=-1, keepdims=True) + 1e-05)).astype(
        jnp.bfloat16
    )
    logits = jnp.dot(normed, router, preferred_element_type=jnp.float32)
    count_experts = router.shape[1]
    select_experts = (
        expert_ids[:, :, None] == jnp.arange(count_experts, dtype=jnp.int32)[None, None, :]
    )
    chosen = jnp.sum(jnp.where(select_experts, logits[:, None, :], 0.0), axis=-1)
    score = jax.nn.sigmoid(chosen)
    gates = score / jnp.sum(score, axis=1, keepdims=True)
    topk = expert_ids.shape[1]
    capacity = 3 * rows * topk // (2 * n_exp)
    slots = -(-capacity // 16) * 16
    mine = (expert_ids.reshape(-1) == owner).astype(jnp.int32)
    ranks = jnp.cumsum(mine) - mine
    slot_pick = (ranks[None, :] == jnp.arange(slots, dtype=jnp.int32)[:, None]) & (
        mine[None, :] == 1
    )
    slot_pick = slot_pick.astype(jnp.float32).reshape(slots, rows, topk)
    token_pick = jnp.sum(slot_pick, axis=2).astype(jnp.bfloat16)
    slot_rows = jnp.dot(token_pick, normed, preferred_element_type=jnp.float32).astype(jnp.bfloat16)

    model = normed.shape[1]
    decay_hi = carry_decay.astype(jnp.bfloat16)
    decay_lo = (carry_decay - decay_hi.astype(jnp.float32)).astype(jnp.bfloat16)

    def as_slab(v):
        v = v.reshape(-1)
        r = -(-v.shape[0] // model)
        return jnp.pad(v, (0, r * model - v.shape[0])).reshape(r, model)

    pieces = [
        slot_rows,
        as_slab(out_weight),
        as_slab(local_state.astype(jnp.bfloat16)),
        as_slab(jnp.concatenate([decay_hi, decay_lo])),
    ]
    sizes = [p.shape[0] for p in pieces]
    slab = jnp.concatenate(pieces)
    total = slab.shape[0]
    padded = -(-total // 16) * 16
    slab = jnp.pad(slab, ((0, padded - total), (0, 0)))
    gathered = lax.all_gather(slab, "seq", axis=0, tiled=False)
    offsets = [sum(sizes[:i]) for i in range(len(sizes))]
    gathered_rows = gathered[:, offsets[0] : offsets[0] + sizes[0]].reshape(n_seq * slots, model)
    full_weight = (
        gathered[:, offsets[1] : offsets[1] + sizes[1]]
        .reshape(n_seq, -1)[:, : out_weight.size]
        .reshape(n_seq * out_weight.shape[0], out_weight.shape[1])
    )
    states = (
        gathered[:, offsets[2] : offsets[2] + sizes[2]]
        .reshape(n_seq, -1)[:, : local_state.size]
        .reshape(n_seq, heads_here, width, width)
    )
    decays = gathered[:, offsets[3], : 2 * heads_here].astype(jnp.float32)
    decays = decays[:, :heads_here] + decays[:, heads_here:]

    blocks = jnp.arange(n_seq)
    between = (blocks[:, None] < blocks[None, :]) & (blocks[None, :] < me_seq)
    factors = jnp.where(between[:, :, None], decays[None, :, :], 1.0)
    reach = jnp.where((blocks < me_seq)[:, None], jnp.prod(factors, axis=1), 0.0)
    state_in = jnp.einsum(
        "jh,jhde->hde", reach, states.astype(jnp.float32), precision=lax.Precision.HIGHEST
    )

    lower = jnp.arange(rows)[:, None] >= jnp.arange(rows)[None, :]
    diff = cum[:, :, None] - cum[:, None, :]
    weight = jnp.where(lower[None], jnp.exp(jnp.where(lower[None], diff, 0.0)), 0.0)
    scores = jnp.einsum("hid,hjd->hij", qloc, kloc, precision=lax.Precision.HIGHEST) * weight
    inner = jnp.einsum("hij,hjd->hid", scores, vloc, precision=lax.Precision.HIGHEST)
    outer = jnp.exp(cum)[:, :, None] * jnp.einsum(
        "hid,hde->hie", qloc, state_in, precision=lax.Precision.HIGHEST
    )
    mixed = inner + outer
    mixed = mixed * lax.rsqrt(jnp.mean(mixed * mixed, axis=-1, keepdims=True) + 1e-06)
    attn = mixed.transpose(1, 0, 2).reshape(rows, heads_here * width).astype(jnp.bfloat16)

    projected = lax.dot_general(
        attn, full_weight, (((1,), (1,)), ((), ())), preferred_element_type=jnp.float32
    )
    hidden = jax.nn.silu(
        jnp.dot(gathered_rows, up_weight[0], preferred_element_type=jnp.float32)
    ).astype(jnp.bfloat16)
    expert_part = jnp.dot(hidden, down_weight[0], preferred_element_type=jnp.float32)
    expert_out = ring_scatter(expert_part.reshape(n_seq, slots, -1), "seq")
    combine = jnp.einsum("cbk,bk->bc", slot_pick, gates, precision=lax.Precision.HIGHEST)
    contribution = jnp.dot(combine, expert_out, precision=lax.Precision.HIGHEST)
    partial = (projected + contribution).reshape(n_exp, rows // n_exp, -1)
    summed = halving_scatter(partial, "exp")
    own_rows = summed.shape[0]
    own = lax.dynamic_slice_in_dim(stream, owner * own_rows, own_rows, 0)
    return (own + summed).astype(jnp.bfloat16)


def solution(mesh):
    in_specs = (
        P("seq", "exp"),
        P("seq", "exp"),
        P("seq", "exp"),
        P("exp", "seq"),
        P("seq", None),
        P("seq", "exp"),
        P(),
        P("seq", None),
        P("exp", None, "seq"),
        P("exp", "seq", None),
    )
    out_specs = P(("seq", "exp"), None)
    return jax.shard_map(shards, mesh=mesh, in_specs=in_specs, out_specs=out_specs, check_vma=False)
```

```python
import jax
import jax.numpy as jnp
from jax import lax
from jax.sharding import PartitionSpec as P


def halving_scatter(x, axis):
    n = x.shape[1]
    me = lax.axis_index(axis)
    buf = x
    for k in range(n.bit_length() - 1):
        half = buf.reshape(buf.shape[0], 2, buf.shape[1] // 2, *buf.shape[2:])
        upper = ((me >> k) & 1) == 1
        keep = jnp.where(upper, half[:, 1], half[:, 0])
        send = jnp.where(upper, half[:, 0], half[:, 1])
        got = lax.ppermute(send.astype(jnp.bfloat16), axis, [(i, i ^ (1 << k)) for i in range(n)])
        buf = keep + got.astype(keep.dtype)
    return buf[:, 0]


def bit_reversed(n):
    bits = n.bit_length() - 1
    return [int(format(i, f"0{bits}b")[::-1], 2) for i in range(n)]


def shards(
    queries,
    key_matrix,
    values,
    log_decay,
    residual,
    out_weight,
    router,
    expert_ids,
    up_weight,
    down_weight,
):
    rows = queries.shape[0]
    heads_here = log_decay.shape[0]
    width = queries.shape[1] // heads_here
    n_seq = lax.axis_size("seq")
    n_exp = lax.axis_size("exp")
    me_seq = lax.axis_index("seq")
    owner = lax.axis_index("exp")

    def split_heads(array):
        return array.astype(jnp.float32).reshape(rows, heads_here, width).transpose(1, 0, 2)

    qloc = split_heads(queries)
    kloc = split_heads(key_matrix)
    vloc = split_heads(values)
    upto = (jnp.arange(rows)[:, None] <= jnp.arange(rows)[None, :]).astype(jnp.float32)
    cum = jnp.dot(log_decay, upto, precision=lax.Precision.HIGHEST)
    last = cum[:, -1:]
    carry_decay = jnp.exp(last[:, 0])
    kscaled = kloc * jnp.exp(last - cum)[:, :, None]
    local_state = jnp.einsum("hjd,hje->hde", kscaled, vloc, precision=lax.Precision.HIGHEST)

    stream = residual.astype(jnp.float32)
    normed = (stream * lax.rsqrt(jnp.mean(stream * stream, axis=-1, keepdims=True) + 1e-05)).astype(
        jnp.bfloat16
    )
    logits = jnp.dot(normed, router, preferred_element_type=jnp.float32)
    count_experts = router.shape[1]
    select_experts = (
        expert_ids[:, :, None] == jnp.arange(count_experts, dtype=jnp.int32)[None, None, :]
    )
    chosen = jnp.sum(jnp.where(select_experts, logits[:, None, :], 0.0), axis=-1)
    score = jax.nn.sigmoid(chosen)
    gates = score / jnp.sum(score, axis=1, keepdims=True)
    topk = expert_ids.shape[1]
    capacity = 3 * rows * topk // (2 * n_exp)
    slots = -(-capacity // 16) * 16
    mine = (expert_ids.reshape(-1) == owner).astype(jnp.int32)
    pairs = mine.shape[0]
    before = (jnp.arange(pairs)[:, None] < jnp.arange(pairs)[None, :]).astype(jnp.bfloat16)
    ranks = jnp.dot(mine.astype(jnp.bfloat16), before, preferred_element_type=jnp.float32).astype(jnp.int32)
    slot_pick = (ranks[None, :] == jnp.arange(slots, dtype=jnp.int32)[:, None]) & (
        mine[None, :] == 1
    )
    slot_pick = slot_pick.astype(jnp.float32).reshape(slots, rows, topk)
    token_pick = jnp.sum(slot_pick, axis=2).astype(jnp.bfloat16)
    slot_rows = jnp.dot(token_pick, normed, preferred_element_type=jnp.float32).astype(jnp.bfloat16)

    model = normed.shape[1]
    decay_hi = carry_decay.astype(jnp.bfloat16)
    decay_lo = (carry_decay - decay_hi.astype(jnp.float32)).astype(jnp.bfloat16)

    def as_slab(v):
        v = v.reshape(-1)
        r = -(-v.shape[0] // model)
        return jnp.pad(v, (0, r * model - v.shape[0])).reshape(r, model)

    pieces = [
        slot_rows,
        as_slab(out_weight),
        as_slab(local_state.astype(jnp.bfloat16)),
        as_slab(jnp.concatenate([decay_hi, decay_lo])),
    ]
    sizes = [p.shape[0] for p in pieces]
    slab = jnp.concatenate(pieces)
    total = slab.shape[0]
    padded = -(-total // 16) * 16
    slab = jnp.pad(slab, ((0, padded - total), (0, 0)))
    gathered = lax.all_gather(slab, "seq", axis=0, tiled=False)
    offsets = [sum(sizes[:i]) for i in range(len(sizes))]
    gathered_rows = gathered[:, offsets[0] : offsets[0] + sizes[0]].reshape(n_seq * slots, model)
    full_weight = (
        gathered[:, offsets[1] : offsets[1] + sizes[1]]
        .reshape(n_seq, -1)[:, : out_weight.size]
        .reshape(n_seq * out_weight.shape[0], out_weight.shape[1])
    )
    states = (
        gathered[:, offsets[2] : offsets[2] + sizes[2]]
        .reshape(n_seq, -1)[:, : local_state.size]
        .reshape(n_seq, heads_here, width, width)
    )
    decays = gathered[:, offsets[3], : 2 * heads_here].astype(jnp.float32)
    decays = decays[:, :heads_here] + decays[:, heads_here:]

    blocks = jnp.arange(n_seq)
    between = (blocks[:, None] < blocks[None, :]) & (blocks[None, :] < me_seq)
    factors = jnp.where(between[:, :, None], decays[None, :, :], 1.0)
    reach = jnp.where((blocks < me_seq)[:, None], jnp.prod(factors, axis=1), 0.0)
    state_in = jnp.einsum(
        "jh,jhde->hde", reach, states.astype(jnp.float32), precision=lax.Precision.HIGHEST
    )

    lower = jnp.arange(rows)[:, None] >= jnp.arange(rows)[None, :]
    diff = cum[:, :, None] - cum[:, None, :]
    weight = jnp.where(lower[None], jnp.exp(jnp.where(lower[None], diff, 0.0)), 0.0)
    scores = jnp.einsum("hid,hjd->hij", qloc, kloc, precision=lax.Precision.HIGHEST) * weight
    inner = jnp.einsum("hij,hjd->hid", scores, vloc, precision=lax.Precision.HIGHEST)
    outer = jnp.exp(cum)[:, :, None] * jnp.einsum(
        "hid,hde->hie", qloc, state_in, precision=lax.Precision.HIGHEST
    )
    mixed = inner + outer
    mixed = mixed * lax.rsqrt(jnp.mean(mixed * mixed, axis=-1, keepdims=True) + 1e-06)
    attn = mixed.transpose(1, 0, 2).reshape(rows, heads_here * width).astype(jnp.bfloat16)

    per = rows // n_exp
    order = bit_reversed(n_exp)

    def chunk_order(a):
        return a.reshape(n_exp, per, -1).transpose(1, 0, 2)[:, order].reshape(rows, -1)

    projected = lax.dot_general(
        chunk_order(attn), full_weight, (((1,), (1,)), ((), ())), preferred_element_type=jnp.float32
    )
    hidden = jax.nn.silu(
        jnp.dot(gathered_rows, up_weight[0], preferred_element_type=jnp.float32)
    ).astype(jnp.bfloat16)
    expert_part = jnp.dot(hidden, down_weight[0], preferred_element_type=jnp.float32)
    expert_out = lax.psum_scatter(
        expert_part.astype(jnp.bfloat16).reshape(n_seq, slots, -1),
        "seq",
        scatter_dimension=0,
        tiled=True,
    )[0]
    combine = chunk_order(jnp.einsum("cbk,bk->bc", slot_pick, gates, precision=lax.Precision.HIGHEST))
    combine_hi = combine.astype(jnp.bfloat16)
    combine_lo = (combine - combine_hi.astype(jnp.float32)).astype(jnp.bfloat16)
    contribution = jnp.dot(combine_hi, expert_out, preferred_element_type=jnp.float32) + jnp.dot(
        combine_lo, expert_out, preferred_element_type=jnp.float32
    )
    partial = (projected + contribution).reshape(per, n_exp, -1)
    summed = halving_scatter(partial, "exp")
    own_rows = summed.shape[0]
    own = lax.dynamic_slice_in_dim(stream, owner * own_rows, own_rows, 0)
    return (own + summed).astype(jnp.bfloat16)


def solution(mesh):
    in_specs = (
        P("seq", "exp"),
        P("seq", "exp"),
        P("seq", "exp"),
        P("exp", "seq"),
        P("seq", None),
        P("seq", "exp"),
        P(),
        P("seq", None),
        P("exp", None, "seq"),
        P("exp", "seq", None),
    )
    out_specs = P(("seq", "exp"), None)
    return jax.shard_map(shards, mesh=mesh, in_specs=in_specs, out_specs=out_specs, check_vma=False)
```

```python
import jax
import jax.numpy as jnp
from jax import lax
from jax.sharding import PartitionSpec as P


def ring_label(n):
    if n != 32:
        return list(range(n))

    def gray(v):
        return v ^ (v >> 1)

    return [gray(e >> 3) * 8 + gray((e >> 1) & 3) * 2 + (e & 1) for e in range(n)]


def halving_scatter(x, axis):
    n = x.shape[1]
    label = ring_label(n)
    member_of = {v: e for e, v in enumerate(label)}
    me = lax.axis_index(axis)
    mine = jnp.asarray(label, jnp.int32)[me]
    buf = x
    for k in range(n.bit_length() - 1):
        half = buf.reshape(buf.shape[0], 2, buf.shape[1] // 2, *buf.shape[2:])
        upper = ((mine >> k) & 1) == 1
        keep = jnp.where(upper, half[:, 1], half[:, 0])
        send = jnp.where(upper, half[:, 0], half[:, 1])
        pairs = [(e, member_of[label[e] ^ (1 << k)]) for e in range(n)]
        got = lax.ppermute(send.astype(jnp.bfloat16), axis, pairs)
        buf = keep + got.astype(keep.dtype)
    return buf[:, 0]


def chunk_positions(n):
    bits = n.bit_length() - 1
    member_of = {v: e for e, v in enumerate(ring_label(n))}
    return [member_of[int(format(p, f"0{bits}b")[::-1], 2)] for p in range(n)]


def shards(
    queries,
    key_matrix,
    values,
    log_decay,
    residual,
    out_weight,
    router,
    expert_ids,
    up_weight,
    down_weight,
):
    rows = queries.shape[0]
    heads_here = log_decay.shape[0]
    width = queries.shape[1] // heads_here
    n_seq = lax.axis_size("seq")
    n_exp = lax.axis_size("exp")
    me_seq = lax.axis_index("seq")
    owner = lax.axis_index("exp")

    def split_heads(array):
        return array.astype(jnp.float32).reshape(rows, heads_here, width).transpose(1, 0, 2)

    qloc = split_heads(queries)
    kloc = split_heads(key_matrix)
    vloc = split_heads(values)
    upto = (jnp.arange(rows)[:, None] <= jnp.arange(rows)[None, :]).astype(jnp.float32)
    cum = jnp.dot(log_decay, upto, precision=lax.Precision.HIGHEST)
    last = cum[:, -1:]
    carry_decay = jnp.exp(last[:, 0])
    kscaled = kloc * jnp.exp(last - cum)[:, :, None]
    local_state = jnp.einsum("hjd,hje->hde", kscaled, vloc, precision=lax.Precision.HIGHEST)

    stream = residual.astype(jnp.float32)
    normed = (stream * lax.rsqrt(jnp.mean(stream * stream, axis=-1, keepdims=True) + 1e-05)).astype(
        jnp.bfloat16
    )
    logits = jnp.dot(normed, router, preferred_element_type=jnp.float32)
    count_experts = router.shape[1]
    select_experts = (
        expert_ids[:, :, None] == jnp.arange(count_experts, dtype=jnp.int32)[None, None, :]
    )
    chosen = jnp.sum(jnp.where(select_experts, logits[:, None, :], 0.0), axis=-1)
    score = jax.nn.sigmoid(chosen)
    gates = score / jnp.sum(score, axis=1, keepdims=True)
    topk = expert_ids.shape[1]
    capacity = 3 * rows * topk // (2 * n_exp)
    slots = -(-capacity // 16) * 16
    mine = (expert_ids.reshape(-1) == owner).astype(jnp.int32)
    pairs = mine.shape[0]
    before = (jnp.arange(pairs)[:, None] < jnp.arange(pairs)[None, :]).astype(jnp.bfloat16)
    ranks = jnp.dot(mine.astype(jnp.bfloat16), before, preferred_element_type=jnp.float32).astype(jnp.int32)
    slot_pick = (ranks[None, :] == jnp.arange(slots, dtype=jnp.int32)[:, None]) & (
        mine[None, :] == 1
    )
    slot_pick = slot_pick.astype(jnp.float32).reshape(slots, rows, topk)
    token_pick = jnp.sum(slot_pick, axis=2).astype(jnp.bfloat16)
    slot_rows = jnp.dot(token_pick, normed, preferred_element_type=jnp.float32).astype(jnp.bfloat16)

    model = normed.shape[1]
    decay_hi = carry_decay.astype(jnp.bfloat16)
    decay_lo = (carry_decay - decay_hi.astype(jnp.float32)).astype(jnp.bfloat16)

    def as_slab(v):
        v = v.reshape(-1)
        r = -(-v.shape[0] // model)
        return jnp.pad(v, (0, r * model - v.shape[0])).reshape(r, model)

    pieces = [
        slot_rows,
        as_slab(out_weight),
        as_slab(local_state.astype(jnp.bfloat16)),
        as_slab(jnp.concatenate([decay_hi, decay_lo])),
    ]
    sizes = [p.shape[0] for p in pieces]
    slab = jnp.concatenate(pieces)
    total = slab.shape[0]
    padded = -(-total // 16) * 16
    slab = jnp.pad(slab, ((0, padded - total), (0, 0)))
    gathered = lax.all_gather(slab, "seq", axis=0, tiled=False)
    offsets = [sum(sizes[:i]) for i in range(len(sizes))]
    gathered_rows = gathered[:, offsets[0] : offsets[0] + sizes[0]].reshape(n_seq * slots, model)
    full_weight = (
        gathered[:, offsets[1] : offsets[1] + sizes[1]]
        .reshape(n_seq, -1)[:, : out_weight.size]
        .reshape(n_seq * out_weight.shape[0], out_weight.shape[1])
    )
    states = (
        gathered[:, offsets[2] : offsets[2] + sizes[2]]
        .reshape(n_seq, -1)[:, : local_state.size]
        .reshape(n_seq, heads_here, width, width)
    )
    decays = gathered[:, offsets[3], : 2 * heads_here].astype(jnp.float32)
    decays = decays[:, :heads_here] + decays[:, heads_here:]

    blocks = jnp.arange(n_seq)
    between = (blocks[:, None] < blocks[None, :]) & (blocks[None, :] < me_seq)
    factors = jnp.where(between[:, :, None], decays[None, :, :], 1.0)
    reach = jnp.where((blocks < me_seq)[:, None], jnp.prod(factors, axis=1), 0.0)
    state_in = jnp.einsum(
        "jh,jhde->hde", reach, states.astype(jnp.float32), precision=lax.Precision.HIGHEST
    )

    lower = jnp.arange(rows)[:, None] >= jnp.arange(rows)[None, :]
    diff = cum[:, :, None] - cum[:, None, :]
    weight = jnp.where(lower[None], jnp.exp(jnp.where(lower[None], diff, 0.0)), 0.0)
    scores = jnp.einsum("hid,hjd->hij", qloc, kloc, precision=lax.Precision.HIGHEST) * weight
    inner = jnp.einsum("hij,hjd->hid", scores, vloc, precision=lax.Precision.HIGHEST)
    outer = jnp.exp(cum)[:, :, None] * jnp.einsum(
        "hid,hde->hie", qloc, state_in, precision=lax.Precision.HIGHEST
    )
    mixed = inner + outer
    mixed = mixed * lax.rsqrt(jnp.mean(mixed * mixed, axis=-1, keepdims=True) + 1e-06)
    attn = mixed.transpose(1, 0, 2).reshape(rows, heads_here * width).astype(jnp.bfloat16)

    per = rows // n_exp
    order = chunk_positions(n_exp)

    def chunk_order(a):
        return a.reshape(n_exp, per, -1).transpose(1, 0, 2)[:, order].reshape(rows, -1)

    projected = lax.dot_general(
        chunk_order(attn), full_weight, (((1,), (1,)), ((), ())), preferred_element_type=jnp.float32
    )
    hidden = jax.nn.silu(
        jnp.dot(gathered_rows, up_weight[0], preferred_element_type=jnp.float32)
    ).astype(jnp.bfloat16)
    expert_part = jnp.dot(hidden, down_weight[0], preferred_element_type=jnp.float32)
    expert_out = lax.psum_scatter(
        expert_part.astype(jnp.bfloat16).reshape(n_seq, slots, -1),
        "seq",
        scatter_dimension=0,
        tiled=True,
    )[0]
    combine = chunk_order(jnp.einsum("cbk,bk->bc", slot_pick, gates, precision=lax.Precision.HIGHEST))
    combine_hi = combine.astype(jnp.bfloat16)
    combine_lo = (combine - combine_hi.astype(jnp.float32)).astype(jnp.bfloat16)
    contribution = jnp.dot(combine_hi, expert_out, preferred_element_type=jnp.float32) + jnp.dot(
        combine_lo, expert_out, preferred_element_type=jnp.float32
    )
    partial = (projected + contribution).reshape(per, n_exp, -1)
    summed = halving_scatter(partial, "exp")
    own_rows = summed.shape[0]
    own = lax.dynamic_slice_in_dim(stream, owner * own_rows, own_rows, 0)
    return (own + summed).astype(jnp.bfloat16)


def solution(mesh):
    in_specs = (
        P("seq", "exp"),
        P("seq", "exp"),
        P("seq", "exp"),
        P("exp", "seq"),
        P("seq", None),
        P("seq", "exp"),
        P(),
        P("seq", None),
        P("exp", None, "seq"),
        P("exp", "seq", None),
    )
    out_specs = P(("seq", "exp"), None)
    return jax.shard_map(shards, mesh=mesh, in_specs=in_specs, out_specs=out_specs, check_vma=False)
```

```python
import jax
import jax.numpy as jnp
from jax import lax
from jax.sharding import PartitionSpec as P


def ring_label(n):
    if n != 32:
        return list(range(n))

    def gray(v):
        return v ^ (v >> 1)

    return [gray(e >> 3) * 8 + gray((e >> 1) & 3) * 2 + (e & 1) for e in range(n)]


def halving_scatter(x, axis):
    n = x.shape[1]
    label = ring_label(n)
    member_of = {v: e for e, v in enumerate(label)}
    me = lax.axis_index(axis)
    mine = jnp.asarray(label, jnp.int32)[me]
    buf = x
    for k in range(n.bit_length() - 1):
        half = buf.reshape(buf.shape[0], 2, buf.shape[1] // 2, *buf.shape[2:])
        upper = ((mine >> k) & 1) == 1
        keep = jnp.where(upper, half[:, 1], half[:, 0])
        send = jnp.where(upper, half[:, 0], half[:, 1])
        pairs = [(e, member_of[label[e] ^ (1 << k)]) for e in range(n)]
        got = lax.ppermute(send.astype(jnp.bfloat16), axis, pairs)
        buf = keep + got.astype(keep.dtype)
    return buf[:, 0]


def chunk_positions(n):
    bits = n.bit_length() - 1
    member_of = {v: e for e, v in enumerate(ring_label(n))}
    return [member_of[int(format(p, f"0{bits}b")[::-1], 2)] for p in range(n)]


def state_prefix(decay, state, axis):
    n = lax.axis_size(axis)
    me = lax.axis_index(axis)
    heads, width = state.shape[0], state.shape[1]
    pack = jnp.concatenate([state, jnp.broadcast_to(decay[:, None, None], (heads, 8, width))], axis=1)
    got = lax.ppermute(pack, axis, [(i, i + 1) for i in range(n - 1)])
    pack = jnp.where(me == 0, jnp.concatenate([jnp.zeros_like(state), jnp.ones((heads, 8, width), state.dtype)], axis=1), got)
    shift = 1
    while shift < n:
        got = lax.ppermute(pack, axis, [(i, i + shift) for i in range(n - shift)])
        d_mine = pack[:, width:width + 1, :]
        fresh = jnp.concatenate([d_mine * got[:, :width] + pack[:, :width], d_mine * got[:, width:]], axis=1)
        pack = jnp.where(me >= shift, fresh, pack)
        shift *= 2
    return pack[:, :width]


def shards(
    queries,
    key_matrix,
    values,
    log_decay,
    residual,
    out_weight,
    router,
    expert_ids,
    up_weight,
    down_weight,
):
    rows = queries.shape[0]
    heads_here = log_decay.shape[0]
    width = queries.shape[1] // heads_here
    n_seq = lax.axis_size("seq")
    n_exp = lax.axis_size("exp")
    me_seq = lax.axis_index("seq")
    owner = lax.axis_index("exp")

    def split_heads(array):
        return array.astype(jnp.float32).reshape(rows, heads_here, width).transpose(1, 0, 2)

    qloc = split_heads(queries)
    kloc = split_heads(key_matrix)
    vloc = split_heads(values)
    upto = (jnp.arange(rows)[:, None] <= jnp.arange(rows)[None, :]).astype(jnp.float32)
    cum = jnp.dot(log_decay, upto, precision=lax.Precision.HIGHEST)
    last = cum[:, -1:]
    carry_decay = jnp.exp(last[:, 0])
    kscaled = kloc * jnp.exp(last - cum)[:, :, None]
    local_state = jnp.einsum("hjd,hje->hde", kscaled, vloc, precision=lax.Precision.HIGHEST)

    stream = residual.astype(jnp.float32)
    normed = (stream * lax.rsqrt(jnp.mean(stream * stream, axis=-1, keepdims=True) + 1e-05)).astype(
        jnp.bfloat16
    )
    logits = jnp.dot(normed, router, preferred_element_type=jnp.float32)
    count_experts = router.shape[1]
    select_experts = (
        expert_ids[:, :, None] == jnp.arange(count_experts, dtype=jnp.int32)[None, None, :]
    )
    chosen = jnp.sum(jnp.where(select_experts, logits[:, None, :], 0.0), axis=-1)
    score = jax.nn.sigmoid(chosen)
    gates = score / jnp.sum(score, axis=1, keepdims=True)
    topk = expert_ids.shape[1]
    capacity = 3 * rows * topk // (2 * n_exp)
    slots = -(-capacity // 16) * 16
    mine = (expert_ids.reshape(-1) == owner).astype(jnp.int32)
    pairs = mine.shape[0]
    before = (jnp.arange(pairs)[:, None] < jnp.arange(pairs)[None, :]).astype(jnp.bfloat16)
    ranks = jnp.dot(mine.astype(jnp.bfloat16), before, preferred_element_type=jnp.float32).astype(jnp.int32)
    slot_pick = (ranks[None, :] == jnp.arange(slots, dtype=jnp.int32)[:, None]) & (
        mine[None, :] == 1
    )
    slot_pick = slot_pick.astype(jnp.float32).reshape(slots, rows, topk)
    token_pick = jnp.sum(slot_pick, axis=2).astype(jnp.bfloat16)
    slot_rows = jnp.dot(token_pick, normed, preferred_element_type=jnp.float32).astype(jnp.bfloat16)

    model = normed.shape[1]

    def as_slab(v):
        v = v.reshape(-1)
        r = -(-v.shape[0] // model)
        return jnp.pad(v, (0, r * model - v.shape[0])).reshape(r, model)

    pieces = [slot_rows, as_slab(out_weight)]
    sizes = [p.shape[0] for p in pieces]
    slab = jnp.concatenate(pieces)
    total = slab.shape[0]
    padded = -(-total // 16) * 16
    slab = jnp.pad(slab, ((0, padded - total), (0, 0)))
    gathered = lax.all_gather(slab, "seq", axis=0, tiled=False)
    offsets = [sum(sizes[:i]) for i in range(len(sizes))]
    gathered_rows = gathered[:, offsets[0] : offsets[0] + sizes[0]].reshape(n_seq * slots, model)
    full_weight = (
        gathered[:, offsets[1] : offsets[1] + sizes[1]]
        .reshape(n_seq, -1)[:, : out_weight.size]
        .reshape(n_seq * out_weight.shape[0], out_weight.shape[1])
    )
    state_in = state_prefix(carry_decay, local_state, "seq")

    lower = jnp.arange(rows)[:, None] >= jnp.arange(rows)[None, :]
    diff = cum[:, :, None] - cum[:, None, :]
    weight = jnp.where(lower[None], jnp.exp(jnp.where(lower[None], diff, 0.0)), 0.0)
    scores = jnp.einsum("hid,hjd->hij", qloc, kloc, precision=lax.Precision.HIGHEST) * weight
    inner = jnp.einsum("hij,hjd->hid", scores, vloc, precision=lax.Precision.HIGHEST)
    outer = jnp.exp(cum)[:, :, None] * jnp.einsum(
        "hid,hde->hie", qloc, state_in, precision=lax.Precision.HIGHEST
    )
    mixed = inner + outer
    mixed = mixed * lax.rsqrt(jnp.mean(mixed * mixed, axis=-1, keepdims=True) + 1e-06)
    attn = mixed.transpose(1, 0, 2).reshape(rows, heads_here * width).astype(jnp.bfloat16)

    per = rows // n_exp
    order = chunk_positions(n_exp)

    def chunk_order(a):
        return a.reshape(n_exp, per, -1).transpose(1, 0, 2)[:, order].reshape(rows, -1)

    projected = lax.dot_general(
        chunk_order(attn), full_weight, (((1,), (1,)), ((), ())), preferred_element_type=jnp.float32
    )
    hidden = jax.nn.silu(
        jnp.dot(gathered_rows, up_weight[0], preferred_element_type=jnp.float32)
    ).astype(jnp.bfloat16)
    expert_part = jnp.dot(hidden, down_weight[0], preferred_element_type=jnp.float32)
    expert_out = lax.psum_scatter(
        expert_part.astype(jnp.bfloat16).reshape(n_seq, slots, -1),
        "seq",
        scatter_dimension=0,
        tiled=True,
    )[0]
    combine = chunk_order(jnp.einsum("cbk,bk->bc", slot_pick, gates, precision=lax.Precision.HIGHEST))
    combine_hi = combine.astype(jnp.bfloat16)
    combine_lo = (combine - combine_hi.astype(jnp.float32)).astype(jnp.bfloat16)
    contribution = jnp.dot(combine_hi, expert_out, preferred_element_type=jnp.float32) + jnp.dot(
        combine_lo, expert_out, preferred_element_type=jnp.float32
    )
    partial = (projected + contribution).reshape(per, n_exp, -1)
    summed = halving_scatter(partial, "exp")
    own_rows = summed.shape[0]
    own = lax.dynamic_slice_in_dim(stream, owner * own_rows, own_rows, 0)
    return (own + summed).astype(jnp.bfloat16)


def solution(mesh):
    in_specs = (
        P("seq", "exp"),
        P("seq", "exp"),
        P("seq", "exp"),
        P("exp", "seq"),
        P("seq", None),
        P("seq", "exp"),
        P(),
        P("seq", None),
        P("exp", None, "seq"),
        P("exp", "seq", None),
    )
    out_specs = P(("seq", "exp"), None)
    return jax.shard_map(shards, mesh=mesh, in_specs=in_specs, out_specs=out_specs, check_vma=False)
```

```python
import jax
import jax.numpy as jnp
from jax import lax
from jax.sharding import PartitionSpec as P


def ring_label(n):
    if n != 32:
        return list(range(n))

    def gray(v):
        return v ^ (v >> 1)

    return [gray(e >> 3) * 8 + gray((e >> 1) & 3) * 2 + (e & 1) for e in range(n)]


def halving_scatter(x, axis):
    n = x.shape[1]
    label = ring_label(n)
    member_of = {v: e for e, v in enumerate(label)}
    me = lax.axis_index(axis)
    mine = jnp.asarray(label, jnp.int32)[me]
    buf = x
    for k in range(n.bit_length() - 1):
        half = buf.reshape(buf.shape[0], 2, buf.shape[1] // 2, *buf.shape[2:])
        upper = ((mine >> k) & 1) == 1
        keep = jnp.where(upper, half[:, 1], half[:, 0])
        send = jnp.where(upper, half[:, 0], half[:, 1])
        pairs = [(e, member_of[label[e] ^ (1 << k)]) for e in range(n)]
        got = lax.ppermute(send.astype(jnp.bfloat16), axis, pairs)
        buf = keep + got.astype(keep.dtype)
    return buf[:, 0]


def chunk_positions(n):
    bits = n.bit_length() - 1
    member_of = {v: e for e, v in enumerate(ring_label(n))}
    return [member_of[int(format(p, f"0{bits}b")[::-1], 2)] for p in range(n)]


def state_prefix(decay, state, axis):
    n = lax.axis_size(axis)
    me = lax.axis_index(axis)
    heads, width = state.shape[0], state.shape[1]
    pack = jnp.concatenate([state, jnp.broadcast_to(decay[:, None, None], (heads, 8, width))], axis=1)
    got = lax.ppermute(pack, axis, [(i, i + 1) for i in range(n - 1)])
    pack = jnp.where(me == 0, jnp.concatenate([jnp.zeros_like(state), jnp.ones((heads, 8, width), state.dtype)], axis=1), got)
    shift = 1
    while shift < n:
        got = lax.ppermute(pack, axis, [(i, i + shift) for i in range(n - shift)])
        d_mine = pack[:, width:width + 1, :]
        fresh = jnp.concatenate([d_mine * got[:, :width] + pack[:, :width], d_mine * got[:, width:]], axis=1)
        pack = jnp.where(me >= shift, fresh, pack)
        shift *= 2
    return pack[:, :width]


def shards(
    queries,
    key_matrix,
    values,
    log_decay,
    residual,
    out_weight,
    router,
    expert_ids,
    up_weight,
    down_weight,
):
    rows = queries.shape[0]
    heads_here = log_decay.shape[0]
    width = queries.shape[1] // heads_here
    n_seq = lax.axis_size("seq")
    n_exp = lax.axis_size("exp")
    me_seq = lax.axis_index("seq")
    owner = lax.axis_index("exp")

    def split_heads(array):
        return array.astype(jnp.float32).reshape(rows, heads_here, width).transpose(1, 0, 2)

    qloc = split_heads(queries)
    kloc = split_heads(key_matrix)
    vloc = split_heads(values)
    upto = (jnp.arange(rows)[:, None] <= jnp.arange(rows)[None, :]).astype(jnp.float32)
    cum = jnp.dot(log_decay, upto, precision=lax.Precision.HIGHEST)
    last = cum[:, -1:]
    carry_decay = jnp.exp(last[:, 0])
    kscaled = kloc * jnp.exp(last - cum)[:, :, None]
    local_state = jnp.einsum("hjd,hje->hde", kscaled, vloc, precision=lax.Precision.HIGHEST)

    stream = residual.astype(jnp.float32)
    normed = (stream * lax.rsqrt(jnp.mean(stream * stream, axis=-1, keepdims=True) + 1e-05)).astype(
        jnp.bfloat16
    )
    logits = jnp.dot(normed, router, preferred_element_type=jnp.float32)
    count_experts = router.shape[1]
    select_experts = (
        expert_ids[:, :, None] == jnp.arange(count_experts, dtype=jnp.int32)[None, None, :]
    )
    chosen = jnp.sum(jnp.where(select_experts, logits[:, None, :], 0.0), axis=-1)
    score = jax.nn.sigmoid(chosen)
    gates = score / jnp.sum(score, axis=1, keepdims=True)
    topk = expert_ids.shape[1]
    capacity = 3 * rows * topk // (2 * n_exp)
    slots = -(-capacity // 16) * 16
    mine = (expert_ids.reshape(-1) == owner).astype(jnp.int32)
    pairs = mine.shape[0]
    before = (jnp.arange(pairs)[:, None] < jnp.arange(pairs)[None, :]).astype(jnp.bfloat16)
    ranks = jnp.dot(mine.astype(jnp.bfloat16), before, preferred_element_type=jnp.float32).astype(jnp.int32)
    slot_pick = (ranks[None, :] == jnp.arange(slots, dtype=jnp.int32)[:, None]) & (
        mine[None, :] == 1
    )
    slot_pick = slot_pick.astype(jnp.float32).reshape(slots, rows, topk)
    token_pick = jnp.sum(slot_pick, axis=2).astype(jnp.bfloat16)
    slot_rows = jnp.dot(token_pick, normed, preferred_element_type=jnp.float32).astype(jnp.bfloat16)

    model = normed.shape[1]

    def as_slab(v):
        v = v.reshape(-1)
        r = -(-v.shape[0] // model)
        return jnp.pad(v, (0, r * model - v.shape[0])).reshape(r, model)

    pieces = [slot_rows, as_slab(out_weight)]
    sizes = [p.shape[0] for p in pieces]
    slab = jnp.concatenate(pieces)
    total = slab.shape[0]
    padded = -(-total // 16) * 16
    slab = jnp.pad(slab, ((0, padded - total), (0, 0)))
    gathered = lax.all_gather(slab, "seq", axis=0, tiled=False)
    gathered, state_in = lax.optimization_barrier((gathered, state_prefix(carry_decay, local_state, "seq")))
    offsets = [sum(sizes[:i]) for i in range(len(sizes))]
    gathered_rows = gathered[:, offsets[0] : offsets[0] + sizes[0]].reshape(n_seq * slots, model)
    full_weight = (
        gathered[:, offsets[1] : offsets[1] + sizes[1]]
        .reshape(n_seq, -1)[:, : out_weight.size]
        .reshape(n_seq * out_weight.shape[0], out_weight.shape[1])
    )
    lower = jnp.arange(rows)[:, None] >= jnp.arange(rows)[None, :]
    diff = cum[:, :, None] - cum[:, None, :]
    weight = jnp.where(lower[None], jnp.exp(jnp.where(lower[None], diff, 0.0)), 0.0)
    scores = jnp.einsum("hid,hjd->hij", qloc, kloc, precision=lax.Precision.HIGHEST) * weight
    inner = jnp.einsum("hij,hjd->hid", scores, vloc, precision=lax.Precision.HIGHEST)
    outer = jnp.exp(cum)[:, :, None] * jnp.einsum(
        "hid,hde->hie", qloc, state_in, precision=lax.Precision.HIGHEST
    )
    mixed = inner + outer
    mixed = mixed * lax.rsqrt(jnp.mean(mixed * mixed, axis=-1, keepdims=True) + 1e-06)
    attn = mixed.transpose(1, 0, 2).reshape(rows, heads_here * width).astype(jnp.bfloat16)

    per = rows // n_exp
    order = chunk_positions(n_exp)

    def chunk_order(a):
        return a.reshape(n_exp, per, -1).transpose(1, 0, 2)[:, order].reshape(rows, -1)

    projected = lax.dot_general(
        chunk_order(attn), full_weight, (((1,), (1,)), ((), ())), preferred_element_type=jnp.float32
    )
    hidden = jax.nn.silu(
        jnp.dot(gathered_rows, up_weight[0], preferred_element_type=jnp.float32)
    ).astype(jnp.bfloat16)
    expert_part = jnp.dot(hidden, down_weight[0], preferred_element_type=jnp.float32)
    expert_out = lax.psum_scatter(
        expert_part.astype(jnp.bfloat16).reshape(n_seq, slots, -1),
        "seq",
        scatter_dimension=0,
        tiled=True,
    )[0]
    combine = chunk_order(jnp.einsum("cbk,bk->bc", slot_pick, gates, precision=lax.Precision.HIGHEST))
    combine_hi = combine.astype(jnp.bfloat16)
    combine_lo = (combine - combine_hi.astype(jnp.float32)).astype(jnp.bfloat16)
    contribution = jnp.dot(combine_hi, expert_out, preferred_element_type=jnp.float32) + jnp.dot(
        combine_lo, expert_out, preferred_element_type=jnp.float32
    )
    partial = (projected + contribution).reshape(per, n_exp, -1)
    summed = halving_scatter(partial, "exp")
    own_rows = summed.shape[0]
    own = lax.dynamic_slice_in_dim(stream, owner * own_rows, own_rows, 0)
    return (own + summed).astype(jnp.bfloat16)


def solution(mesh):
    in_specs = (
        P("seq", "exp"),
        P("seq", "exp"),
        P("seq", "exp"),
        P("exp", "seq"),
        P("seq", None),
        P("seq", "exp"),
        P(),
        P("seq", None),
        P("exp", None, "seq"),
        P("exp", "seq", None),
    )
    out_specs = P(("seq", "exp"), None)
    return jax.shard_map(shards, mesh=mesh, in_specs=in_specs, out_specs=out_specs, check_vma=False)
```

```python
import jax
import jax.numpy as jnp
from jax import lax
from jax.sharding import PartitionSpec as P


def ring_label(n):
    if n != 32:
        return list(range(n))

    def gray(v):
        return v ^ (v >> 1)

    return [gray(e >> 3) * 8 + gray((e >> 1) & 3) * 2 + (e & 1) for e in range(n)]


def halving_scatter(x, axis):
    n = x.shape[1]
    label = ring_label(n)
    member_of = {v: e for e, v in enumerate(label)}
    me = lax.axis_index(axis)
    mine = jnp.asarray(label, jnp.int32)[me]
    buf = x
    for k in range(n.bit_length() - 1):
        half = buf.reshape(buf.shape[0], 2, buf.shape[1] // 2, *buf.shape[2:])
        upper = ((mine >> k) & 1) == 1
        keep = jnp.where(upper, half[:, 1], half[:, 0])
        send = jnp.where(upper, half[:, 0], half[:, 1])
        pairs = [(e, member_of[label[e] ^ (1 << k)]) for e in range(n)]
        got = lax.ppermute(send.astype(jnp.bfloat16), axis, pairs)
        buf = keep + got.astype(keep.dtype)
    return buf[:, 0]


def chunk_positions(n):
    bits = n.bit_length() - 1
    member_of = {v: e for e, v in enumerate(ring_label(n))}
    return [member_of[int(format(p, f"0{bits}b")[::-1], 2)] for p in range(n)]


def shards(
    queries,
    key_matrix,
    values,
    log_decay,
    residual,
    out_weight,
    router,
    expert_ids,
    up_weight,
    down_weight,
):
    rows = queries.shape[0]
    heads_here = log_decay.shape[0]
    width = queries.shape[1] // heads_here
    n_seq = lax.axis_size("seq")
    n_exp = lax.axis_size("exp")
    me_seq = lax.axis_index("seq")
    owner = lax.axis_index("exp")

    def split_heads(array):
        return array.astype(jnp.float32).reshape(rows, heads_here, width).transpose(1, 0, 2)

    qloc = split_heads(queries)
    kloc = split_heads(key_matrix)
    vloc = split_heads(values)
    upto = (jnp.arange(rows)[:, None] <= jnp.arange(rows)[None, :]).astype(jnp.float32)
    cum = jnp.dot(log_decay, upto, precision=lax.Precision.HIGHEST)
    last = cum[:, -1:]
    carry_decay = jnp.exp(last[:, 0])
    kscaled = kloc * jnp.exp(last - cum)[:, :, None]
    kscaled_hi = kscaled.astype(jnp.bfloat16)
    kscaled_lo = (kscaled - kscaled_hi.astype(jnp.float32)).astype(jnp.bfloat16)
    vbf = values.reshape(rows, heads_here, width).transpose(1, 0, 2)
    local_state = jnp.einsum(
        "hjd,hje->hde", kscaled_hi, vbf, preferred_element_type=jnp.float32
    ) + jnp.einsum("hjd,hje->hde", kscaled_lo, vbf, preferred_element_type=jnp.float32)

    stream = residual.astype(jnp.float32)
    normed = (stream * lax.rsqrt(jnp.mean(stream * stream, axis=-1, keepdims=True) + 1e-05)).astype(
        jnp.bfloat16
    )
    logits = jnp.dot(normed, router, preferred_element_type=jnp.float32)
    count_experts = router.shape[1]
    select_experts = (
        expert_ids[:, :, None] == jnp.arange(count_experts, dtype=jnp.int32)[None, None, :]
    )
    chosen = jnp.sum(jnp.where(select_experts, logits[:, None, :], 0.0), axis=-1)
    score = jax.nn.sigmoid(chosen)
    gates = score / jnp.sum(score, axis=1, keepdims=True)
    topk = expert_ids.shape[1]
    capacity = 3 * rows * topk // (2 * n_exp)
    slots = -(-capacity // 16) * 16
    mine = (expert_ids.reshape(-1) == owner).astype(jnp.int32)
    pairs = mine.shape[0]
    before = (jnp.arange(pairs)[:, None] < jnp.arange(pairs)[None, :]).astype(jnp.bfloat16)
    ranks = jnp.dot(mine.astype(jnp.bfloat16), before, preferred_element_type=jnp.float32).astype(jnp.int32)
    slot_pick = (ranks[None, :] == jnp.arange(slots, dtype=jnp.int32)[:, None]) & (
        mine[None, :] == 1
    )
    slot_pick = slot_pick.astype(jnp.float32).reshape(slots, rows, topk)
    token_pick = jnp.sum(slot_pick, axis=2).astype(jnp.bfloat16)
    slot_rows = jnp.dot(token_pick, normed, preferred_element_type=jnp.float32).astype(jnp.bfloat16)

    model = normed.shape[1]
    decay_hi = carry_decay.astype(jnp.bfloat16)
    decay_lo = (carry_decay - decay_hi.astype(jnp.float32)).astype(jnp.bfloat16)

    def as_slab(v):
        v = v.reshape(-1)
        r = -(-v.shape[0] // model)
        return jnp.pad(v, (0, r * model - v.shape[0])).reshape(r, model)

    pieces = [
        slot_rows,
        as_slab(out_weight),
        as_slab(local_state.astype(jnp.bfloat16)),
        as_slab(jnp.concatenate([decay_hi, decay_lo])),
    ]
    sizes = [p.shape[0] for p in pieces]
    slab = jnp.concatenate(pieces)
    total = slab.shape[0]
    padded = -(-total // 16) * 16
    slab = jnp.pad(slab, ((0, padded - total), (0, 0)))
    gathered = lax.all_gather(slab, "seq", axis=0, tiled=False)
    offsets = [sum(sizes[:i]) for i in range(len(sizes))]
    gathered_rows = gathered[:, offsets[0] : offsets[0] + sizes[0]].reshape(n_seq * slots, model)
    full_weight = (
        gathered[:, offsets[1] : offsets[1] + sizes[1]]
        .reshape(n_seq, -1)[:, : out_weight.size]
        .reshape(n_seq * out_weight.shape[0], out_weight.shape[1])
    )
    states = (
        gathered[:, offsets[2] : offsets[2] + sizes[2]]
        .reshape(n_seq, -1)[:, : local_state.size]
        .reshape(n_seq, heads_here, width, width)
    )
    decays = gathered[:, offsets[3], : 2 * heads_here].astype(jnp.float32)
    decays = decays[:, :heads_here] + decays[:, heads_here:]

    blocks = jnp.arange(n_seq)
    between = (blocks[:, None] < blocks[None, :]) & (blocks[None, :] < me_seq)
    factors = jnp.where(between[:, :, None], decays[None, :, :], 1.0)
    reach = jnp.where((blocks < me_seq)[:, None], jnp.prod(factors, axis=1), 0.0)
    state_in = jnp.einsum(
        "jh,jhde->hde", reach, states.astype(jnp.float32), precision=lax.Precision.HIGHEST
    )

    lower = jnp.arange(rows)[:, None] >= jnp.arange(rows)[None, :]
    diff = cum[:, :, None] - cum[:, None, :]
    weight = jnp.where(lower[None], jnp.exp(jnp.where(lower[None], diff, 0.0)), 0.0)
    scores = jnp.einsum("hid,hjd->hij", qloc, kloc, precision=lax.Precision.HIGHEST) * weight
    inner = jnp.einsum("hij,hjd->hid", scores, vloc, precision=lax.Precision.HIGHEST)
    outer = jnp.exp(cum)[:, :, None] * jnp.einsum(
        "hid,hde->hie", qloc, state_in, precision=lax.Precision.HIGHEST
    )
    mixed = inner + outer
    mixed = mixed * lax.rsqrt(jnp.mean(mixed * mixed, axis=-1, keepdims=True) + 1e-06)
    attn = mixed.transpose(1, 0, 2).reshape(rows, heads_here * width).astype(jnp.bfloat16)

    per = rows // n_exp
    order = chunk_positions(n_exp)

    def chunk_order(a):
        return a.reshape(n_exp, per, -1).transpose(1, 0, 2)[:, order].reshape(rows, -1)

    projected = lax.dot_general(
        chunk_order(attn), full_weight, (((1,), (1,)), ((), ())), preferred_element_type=jnp.float32
    )
    hidden = jax.nn.silu(
        jnp.dot(gathered_rows, up_weight[0], preferred_element_type=jnp.float32)
    ).astype(jnp.bfloat16)
    expert_part = jnp.dot(hidden, down_weight[0], preferred_element_type=jnp.float32)
    expert_out = lax.psum_scatter(
        expert_part.astype(jnp.bfloat16).reshape(n_seq, slots, -1),
        "seq",
        scatter_dimension=0,
        tiled=True,
    )[0]
    combine = chunk_order(jnp.einsum("cbk,bk->bc", slot_pick, gates, precision=lax.Precision.HIGHEST))
    combine_hi = combine.astype(jnp.bfloat16)
    combine_lo = (combine - combine_hi.astype(jnp.float32)).astype(jnp.bfloat16)
    contribution = jnp.dot(combine_hi, expert_out, preferred_element_type=jnp.float32) + jnp.dot(
        combine_lo, expert_out, preferred_element_type=jnp.float32
    )
    partial = (projected + contribution).reshape(per, n_exp, -1)
    summed = halving_scatter(partial, "exp")
    own_rows = summed.shape[0]
    own = lax.dynamic_slice_in_dim(residual, owner * own_rows, own_rows, 0).astype(jnp.float32)
    return (own + summed).astype(jnp.bfloat16)


def solution(mesh):
    in_specs = (
        P("seq", "exp"),
        P("seq", "exp"),
        P("seq", "exp"),
        P("exp", "seq"),
        P("seq", None),
        P("seq", "exp"),
        P(),
        P("seq", None),
        P("exp", None, "seq"),
        P("exp", "seq", None),
    )
    out_specs = P(("seq", "exp"), None)
    return jax.shard_map(shards, mesh=mesh, in_specs=in_specs, out_specs=out_specs, check_vma=False)
```

```python
import jax
import jax.numpy as jnp
from jax import lax
from jax.sharding import PartitionSpec as P


def ring_label(n):
    if n != 32:
        return list(range(n))

    def gray(v):
        return v ^ (v >> 1)

    return [gray((e >> 1) & 3) * 8 + gray(e >> 3) * 2 + (e & 1) for e in range(n)]


def halving_scatter(x, axis):
    n = x.shape[1]
    label = ring_label(n)
    member_of = {v: e for e, v in enumerate(label)}
    me = lax.axis_index(axis)
    mine = jnp.asarray(label, jnp.int32)[me]
    buf = x
    for k in range(n.bit_length() - 1):
        half = buf.reshape(buf.shape[0], 2, buf.shape[1] // 2, *buf.shape[2:])
        upper = ((mine >> k) & 1) == 1
        keep = jnp.where(upper, half[:, 1], half[:, 0])
        send = jnp.where(upper, half[:, 0], half[:, 1])
        pairs = [(e, member_of[label[e] ^ (1 << k)]) for e in range(n)]
        got = lax.ppermute(send.astype(jnp.bfloat16), axis, pairs)
        buf = keep + got.astype(keep.dtype)
    return buf[:, 0]


def chunk_positions(n):
    bits = n.bit_length() - 1
    member_of = {v: e for e, v in enumerate(ring_label(n))}
    return [member_of[int(format(p, f"0{bits}b")[::-1], 2)] for p in range(n)]


def shards(
    queries,
    key_matrix,
    values,
    log_decay,
    residual,
    out_weight,
    router,
    expert_ids,
    up_weight,
    down_weight,
):
    rows = queries.shape[0]
    heads_here = log_decay.shape[0]
    width = queries.shape[1] // heads_here
    n_seq = lax.axis_size("seq")
    n_exp = lax.axis_size("exp")
    me_seq = lax.axis_index("seq")
    owner = lax.axis_index("exp")

    def split_heads(array):
        return array.astype(jnp.float32).reshape(rows, heads_here, width).transpose(1, 0, 2)

    qloc = split_heads(queries)
    kloc = split_heads(key_matrix)
    vloc = split_heads(values)
    upto = (jnp.arange(rows)[:, None] <= jnp.arange(rows)[None, :]).astype(jnp.float32)
    cum = jnp.dot(log_decay, upto, precision=lax.Precision.HIGHEST)
    last = cum[:, -1:]
    carry_decay = jnp.exp(last[:, 0])
    kscaled = kloc * jnp.exp(last - cum)[:, :, None]
    kscaled_hi = kscaled.astype(jnp.bfloat16)
    kscaled_lo = (kscaled - kscaled_hi.astype(jnp.float32)).astype(jnp.bfloat16)
    vbf = values.reshape(rows, heads_here, width).transpose(1, 0, 2)
    local_state = jnp.einsum(
        "hjd,hje->hde", kscaled_hi, vbf, preferred_element_type=jnp.float32
    ) + jnp.einsum("hjd,hje->hde", kscaled_lo, vbf, preferred_element_type=jnp.float32)

    stream = residual.astype(jnp.float32)
    normed = (stream * lax.rsqrt(jnp.mean(stream * stream, axis=-1, keepdims=True) + 1e-05)).astype(
        jnp.bfloat16
    )
    logits = jnp.dot(normed, router, preferred_element_type=jnp.float32)
    count_experts = router.shape[1]
    select_experts = (
        expert_ids[:, :, None] == jnp.arange(count_experts, dtype=jnp.int32)[None, None, :]
    )
    chosen = jnp.sum(jnp.where(select_experts, logits[:, None, :], 0.0), axis=-1)
    score = jax.nn.sigmoid(chosen)
    gates = score / jnp.sum(score, axis=1, keepdims=True)
    topk = expert_ids.shape[1]
    capacity = 3 * rows * topk // (2 * n_exp)
    slots = -(-capacity // 16) * 16
    mine = (expert_ids.reshape(-1) == owner).astype(jnp.int32)
    pairs = mine.shape[0]
    before = (jnp.arange(pairs)[:, None] < jnp.arange(pairs)[None, :]).astype(jnp.bfloat16)
    ranks = jnp.dot(mine.astype(jnp.bfloat16), before, preferred_element_type=jnp.float32).astype(jnp.int32)
    slot_pick = (ranks[None, :] == jnp.arange(slots, dtype=jnp.int32)[:, None]) & (
        mine[None, :] == 1
    )
    slot_pick = slot_pick.astype(jnp.float32).reshape(slots, rows, topk)
    token_pick = jnp.sum(slot_pick, axis=2).astype(jnp.bfloat16)
    slot_rows = jnp.dot(token_pick, normed, preferred_element_type=jnp.float32).astype(jnp.bfloat16)

    model = normed.shape[1]
    decay_hi = carry_decay.astype(jnp.bfloat16)
    decay_lo = (carry_decay - decay_hi.astype(jnp.float32)).astype(jnp.bfloat16)

    def as_slab(v):
        v = v.reshape(-1)
        r = -(-v.shape[0] // model)
        return jnp.pad(v, (0, r * model - v.shape[0])).reshape(r, model)

    pieces = [
        slot_rows,
        as_slab(out_weight),
        as_slab(local_state.astype(jnp.bfloat16)),
        as_slab(jnp.concatenate([decay_hi, decay_lo])),
    ]
    sizes = [p.shape[0] for p in pieces]
    slab = jnp.concatenate(pieces)
    total = slab.shape[0]
    padded = -(-total // 16) * 16
    slab = jnp.pad(slab, ((0, padded - total), (0, 0)))
    gathered = lax.all_gather(slab, "seq", axis=0, tiled=False)
    offsets = [sum(sizes[:i]) for i in range(len(sizes))]
    gathered_rows = gathered[:, offsets[0] : offsets[0] + sizes[0]].reshape(n_seq * slots, model)
    full_weight = (
        gathered[:, offsets[1] : offsets[1] + sizes[1]]
        .reshape(n_seq, -1)[:, : out_weight.size]
        .reshape(n_seq * out_weight.shape[0], out_weight.shape[1])
    )
    states = (
        gathered[:, offsets[2] : offsets[2] + sizes[2]]
        .reshape(n_seq, -1)[:, : local_state.size]
        .reshape(n_seq, heads_here, width, width)
    )
    decays = gathered[:, offsets[3], : 2 * heads_here].astype(jnp.float32)
    decays = decays[:, :heads_here] + decays[:, heads_here:]

    blocks = jnp.arange(n_seq)
    between = (blocks[:, None] < blocks[None, :]) & (blocks[None, :] < me_seq)
    factors = jnp.where(between[:, :, None], decays[None, :, :], 1.0)
    reach = jnp.where((blocks < me_seq)[:, None], jnp.prod(factors, axis=1), 0.0)
    state_in = jnp.einsum(
        "jh,jhde->hde", reach, states.astype(jnp.float32), precision=lax.Precision.HIGHEST
    )

    lower = jnp.arange(rows)[:, None] >= jnp.arange(rows)[None, :]
    diff = cum[:, :, None] - cum[:, None, :]
    weight = jnp.where(lower[None], jnp.exp(jnp.where(lower[None], diff, 0.0)), 0.0)
    scores = jnp.einsum("hid,hjd->hij", qloc, kloc, precision=lax.Precision.HIGHEST) * weight
    inner = jnp.einsum("hij,hjd->hid", scores, vloc, precision=lax.Precision.HIGHEST)
    outer = jnp.exp(cum)[:, :, None] * jnp.einsum(
        "hid,hde->hie", qloc, state_in, precision=lax.Precision.HIGHEST
    )
    mixed = inner + outer
    mixed = mixed * lax.rsqrt(jnp.mean(mixed * mixed, axis=-1, keepdims=True) + 1e-06)
    attn = mixed.transpose(1, 0, 2).reshape(rows, heads_here * width).astype(jnp.bfloat16)

    per = rows // n_exp
    order = chunk_positions(n_exp)

    def chunk_order(a):
        return a.reshape(n_exp, per, -1).transpose(1, 0, 2)[:, order].reshape(rows, -1)

    projected = lax.dot_general(
        chunk_order(attn), full_weight, (((1,), (1,)), ((), ())), preferred_element_type=jnp.float32
    )
    hidden = jax.nn.silu(
        jnp.dot(gathered_rows, up_weight[0], preferred_element_type=jnp.float32)
    ).astype(jnp.bfloat16)
    expert_part = jnp.dot(hidden, down_weight[0], preferred_element_type=jnp.float32)
    expert_out = lax.psum_scatter(
        expert_part.astype(jnp.bfloat16).reshape(n_seq, slots, -1),
        "seq",
        scatter_dimension=0,
        tiled=True,
    )[0]
    combine = chunk_order(jnp.einsum("cbk,bk->bc", slot_pick, gates, precision=lax.Precision.HIGHEST))
    combine_hi = combine.astype(jnp.bfloat16)
    combine_lo = (combine - combine_hi.astype(jnp.float32)).astype(jnp.bfloat16)
    contribution = jnp.dot(combine_hi, expert_out, preferred_element_type=jnp.float32) + jnp.dot(
        combine_lo, expert_out, preferred_element_type=jnp.float32
    )
    partial = (projected + contribution).reshape(per, n_exp, -1)
    summed = halving_scatter(partial, "exp")
    own_rows = summed.shape[0]
    own = lax.dynamic_slice_in_dim(residual, owner * own_rows, own_rows, 0).astype(jnp.float32)
    return (own + summed).astype(jnp.bfloat16)


def solution(mesh):
    in_specs = (
        P("seq", "exp"),
        P("seq", "exp"),
        P("seq", "exp"),
        P("exp", "seq"),
        P("seq", None),
        P("seq", "exp"),
        P(),
        P("seq", None),
        P("exp", None, "seq"),
        P("exp", "seq", None),
    )
    out_specs = P(("seq", "exp"), None)
    return jax.shard_map(shards, mesh=mesh, in_specs=in_specs, out_specs=out_specs, check_vma=False)
```

```python
import jax
import jax.numpy as jnp
from jax import lax
from jax.sharding import PartitionSpec as P


def ring_label(n):
    if n != 32:
        return list(range(n))

    def gray(v):
        return v ^ (v >> 1)

    return [gray((e >> 1) & 3) * 8 + gray(e >> 3) * 2 + (e & 1) for e in range(n)]


def halving_scatter(x, axis):
    n = x.shape[1]
    label = ring_label(n)
    member_of = {v: e for e, v in enumerate(label)}
    me = lax.axis_index(axis)
    mine = jnp.asarray(label, jnp.int32)[me]
    buf = x
    for k in range(n.bit_length() - 1):
        half = buf.reshape(buf.shape[0], 2, buf.shape[1] // 2, *buf.shape[2:])
        upper = ((mine >> k) & 1) == 1
        keep = jnp.where(upper, half[:, 1], half[:, 0])
        send = jnp.where(upper, half[:, 0], half[:, 1])
        pairs = [(e, member_of[label[e] ^ (1 << k)]) for e in range(n)]
        got = lax.ppermute(send.astype(jnp.bfloat16), axis, pairs)
        buf = keep + got.astype(keep.dtype)
    return buf[:, 0]


def chunk_positions(n):
    bits = n.bit_length() - 1
    member_of = {v: e for e, v in enumerate(ring_label(n))}
    return [member_of[int(format(p, f"0{bits}b")[::-1], 2)] for p in range(n)]


def shards(
    queries,
    key_matrix,
    values,
    log_decay,
    residual,
    out_weight,
    router,
    expert_ids,
    up_weight,
    down_weight,
):
    rows = queries.shape[0]
    heads_here = log_decay.shape[0]
    width = queries.shape[1] // heads_here
    n_seq = lax.axis_size("seq")
    n_exp = lax.axis_size("exp")
    me_seq = lax.axis_index("seq")
    owner = lax.axis_index("exp")

    def split_heads(array):
        return array.astype(jnp.float32).reshape(rows, heads_here, width).transpose(1, 0, 2)

    qloc = split_heads(queries)
    kloc = split_heads(key_matrix)
    vloc = split_heads(values)
    upto = (jnp.arange(rows)[:, None] <= jnp.arange(rows)[None, :]).astype(jnp.float32)
    cum = jnp.dot(log_decay, upto, precision=lax.Precision.HIGHEST)
    last = cum[:, -1:]
    carry_decay = jnp.exp(last[:, 0])
    kscaled = kloc * jnp.exp(last - cum)[:, :, None]
    kscaled_hi = kscaled.astype(jnp.bfloat16)
    kscaled_lo = (kscaled - kscaled_hi.astype(jnp.float32)).astype(jnp.bfloat16)
    vbf = values.reshape(rows, heads_here, width).transpose(1, 0, 2)
    local_state = jnp.einsum(
        "hjd,hje->hde", kscaled_hi, vbf, preferred_element_type=jnp.float32
    ) + jnp.einsum("hjd,hje->hde", kscaled_lo, vbf, preferred_element_type=jnp.float32)

    stream = residual.astype(jnp.float32)
    square = stream * stream
    square_hi = square.astype(jnp.bfloat16)
    square_lo = (square - square_hi.astype(jnp.float32)).astype(jnp.bfloat16)
    ones = jnp.ones((stream.shape[1], 128), jnp.bfloat16)
    sums = jnp.dot(square_hi, ones, preferred_element_type=jnp.float32) + jnp.dot(
        square_lo, ones, preferred_element_type=jnp.float32
    )
    mean_square = sums[:, :1] / stream.shape[1]
    normed = (stream * lax.rsqrt(mean_square + 1e-05)).astype(
        jnp.bfloat16
    )
    logits = jnp.dot(normed, router, preferred_element_type=jnp.float32)
    count_experts = router.shape[1]
    select_experts = (
        expert_ids[:, :, None] == jnp.arange(count_experts, dtype=jnp.int32)[None, None, :]
    )
    chosen = jnp.sum(jnp.where(select_experts, logits[:, None, :], 0.0), axis=-1)
    score = jax.nn.sigmoid(chosen)
    gates = score / jnp.sum(score, axis=1, keepdims=True)
    topk = expert_ids.shape[1]
    capacity = 3 * rows * topk // (2 * n_exp)
    slots = -(-capacity // 16) * 16
    mine = (expert_ids.reshape(-1) == owner).astype(jnp.int32)
    pairs = mine.shape[0]
    before = (jnp.arange(pairs)[:, None] < jnp.arange(pairs)[None, :]).astype(jnp.bfloat16)
    ranks = jnp.dot(mine.astype(jnp.bfloat16), before, preferred_element_type=jnp.float32).astype(jnp.int32)
    slot_pick = (ranks[None, :] == jnp.arange(slots, dtype=jnp.int32)[:, None]) & (
        mine[None, :] == 1
    )
    slot_pick = slot_pick.astype(jnp.float32).reshape(slots, rows, topk)
    token_pick = jnp.sum(slot_pick, axis=2).astype(jnp.bfloat16)
    slot_rows = jnp.dot(token_pick, normed, preferred_element_type=jnp.float32).astype(jnp.bfloat16)

    model = normed.shape[1]
    decay_hi = carry_decay.astype(jnp.bfloat16)
    decay_lo = (carry_decay - decay_hi.astype(jnp.float32)).astype(jnp.bfloat16)

    def as_slab(v):
        v = v.reshape(-1)
        r = -(-v.shape[0] // model)
        return jnp.pad(v, (0, r * model - v.shape[0])).reshape(r, model)

    pieces = [
        slot_rows,
        as_slab(out_weight),
        as_slab(local_state.astype(jnp.bfloat16)),
        as_slab(jnp.concatenate([decay_hi, decay_lo])),
    ]
    sizes = [p.shape[0] for p in pieces]
    slab = jnp.concatenate(pieces)
    total = slab.shape[0]
    padded = -(-total // 16) * 16
    slab = jnp.pad(slab, ((0, padded - total), (0, 0)))
    gathered = lax.all_gather(slab, "seq", axis=0, tiled=False)
    offsets = [sum(sizes[:i]) for i in range(len(sizes))]
    gathered_rows = gathered[:, offsets[0] : offsets[0] + sizes[0]].reshape(n_seq * slots, model)
    full_weight = (
        gathered[:, offsets[1] : offsets[1] + sizes[1]]
        .reshape(n_seq, -1)[:, : out_weight.size]
        .reshape(n_seq * out_weight.shape[0], out_weight.shape[1])
    )
    states = (
        gathered[:, offsets[2] : offsets[2] + sizes[2]]
        .reshape(n_seq, -1)[:, : local_state.size]
        .reshape(n_seq, heads_here, width, width)
    )
    decays = gathered[:, offsets[3], : 2 * heads_here].astype(jnp.float32)
    decays = decays[:, :heads_here] + decays[:, heads_here:]

    blocks = jnp.arange(n_seq)
    between = (blocks[:, None] < blocks[None, :]) & (blocks[None, :] < me_seq)
    factors = jnp.where(between[:, :, None], decays[None, :, :], 1.0)
    reach = jnp.where((blocks < me_seq)[:, None], jnp.prod(factors, axis=1), 0.0)
    state_in = jnp.einsum(
        "jh,jhde->hde", reach, states.astype(jnp.float32), precision=lax.Precision.HIGHEST
    )

    lower = jnp.arange(rows)[:, None] >= jnp.arange(rows)[None, :]
    diff = cum[:, :, None] - cum[:, None, :]
    weight = jnp.where(lower[None], jnp.exp(jnp.where(lower[None], diff, 0.0)), 0.0)
    scores = jnp.einsum("hid,hjd->hij", qloc, kloc, precision=lax.Precision.HIGHEST) * weight
    inner = jnp.einsum("hij,hjd->hid", scores, vloc, precision=lax.Precision.HIGHEST)
    outer = jnp.exp(cum)[:, :, None] * jnp.einsum(
        "hid,hde->hie", qloc, state_in, precision=lax.Precision.HIGHEST
    )
    mixed = inner + outer
    mixed = mixed * lax.rsqrt(jnp.mean(mixed * mixed, axis=-1, keepdims=True) + 1e-06)
    attn = mixed.transpose(1, 0, 2).reshape(rows, heads_here * width).astype(jnp.bfloat16)

    per = rows // n_exp
    order = chunk_positions(n_exp)

    def chunk_order(a):
        return a.reshape(n_exp, per, -1).transpose(1, 0, 2)[:, order].reshape(rows, -1)

    projected = lax.dot_general(
        chunk_order(attn), full_weight, (((1,), (1,)), ((), ())), preferred_element_type=jnp.float32
    )
    hidden = jax.nn.silu(
        jnp.dot(gathered_rows, up_weight[0], preferred_element_type=jnp.float32)
    ).astype(jnp.bfloat16)
    expert_part = jnp.dot(hidden, down_weight[0], preferred_element_type=jnp.float32)
    expert_out = lax.psum_scatter(
        expert_part.astype(jnp.bfloat16).reshape(n_seq, slots, -1),
        "seq",
        scatter_dimension=0,
        tiled=True,
    )[0]
    combine = chunk_order(jnp.einsum("cbk,bk->bc", slot_pick, gates, precision=lax.Precision.HIGHEST))
    combine_hi = combine.astype(jnp.bfloat16)
    combine_lo = (combine - combine_hi.astype(jnp.float32)).astype(jnp.bfloat16)
    contribution = jnp.dot(combine_hi, expert_out, preferred_element_type=jnp.float32) + jnp.dot(
        combine_lo, expert_out, preferred_element_type=jnp.float32
    )
    partial = (projected + contribution).reshape(per, n_exp, -1)
    summed = halving_scatter(partial, "exp")
    own_rows = summed.shape[0]
    own = lax.dynamic_slice_in_dim(residual, owner * own_rows, own_rows, 0).astype(jnp.float32)
    return (own + summed).astype(jnp.bfloat16)


def solution(mesh):
    in_specs = (
        P("seq", "exp"),
        P("seq", "exp"),
        P("seq", "exp"),
        P("exp", "seq"),
        P("seq", None),
        P("seq", "exp"),
        P(),
        P("seq", None),
        P("exp", None, "seq"),
        P("exp", "seq", None),
    )
    out_specs = P(("seq", "exp"), None)
    return jax.shard_map(shards, mesh=mesh, in_specs=in_specs, out_specs=out_specs, check_vma=False)
```
